256 devices in a mesh: seq: 64 (over x, z, core), batch: 4 (over y).
Axes of the slice: x: 4, y: 4, z: 8, core: 2. Of those that a mesh axis runs over, the one named last changes fastest.
Arguments:
- token_ids: int32 [4, 16384], P('batch', 'seq'), may hold values from 0 to 15
- input_table: bfloat16 [16, 3840], replicated, may hold values from -6 to 6
- gate_table: bfloat16 [16, 3584], replicated, may hold values from -6 to 6
- step_table: float32 [16, 56], replicated, may hold values from -4.5 to -1.5
- decay_log: float32 [56], replicated, may hold values from -12 to 0
- conv_weight: float32 [4, 3840], replicated, may hold values from -3 to 3
- conv_bias: float32 [3840], replicated, may hold values from -3 to 3
- skip_gain: float32 [56], replicated, may hold values from 0.25 to 1.75
- norm_gain: float32 [3584], replicated, may hold values from 0.5 to 1.5
- cotangent: bfloat16 [4, 16384, 3584], P('batch', 'seq'), may hold values from -1 to 1
Outputs:
- layer_out: bfloat16 [4, 16384, 3584], P('batch', 'seq')
- input_grad: float32 [16, 3840], replicated
- gate_grad: float32 [16, 3584], replicated
- step_grad: float32 [16, 56], replicated
- decay_grad: float32 [56], replicated
- conv_weight_grad: float32 [4, 3840], replicated
- conv_bias_grad: float32 [3840], replicated
- skip_grad: float32 [56], replicated
- norm_grad: float32 [3584], replicated
The draws below stay inside these ranges and needn't reach their ends.
All inputs are finite; a program needn't handle non-finite values.
Results may differ from the reference program's by a relative error of at most 0.014.
Values sent between devices are 32-bit elements; how exact they have to be, the bound alone decides.
No kernel may reach another device: no remote copies, remote signals or barrier semaphores. Data moves between devices by JAX's collectives and lax.ppermute only.
A program may use at most 320 MiB of HBM per device.

```python
import math
from functools import partial
import jax
import jax.numpy as jnp
from jax import lax

VOCAB = 16
HEADS = 56
HEAD = 64
STATE = 128
CONV_WIDTH = 4
BLOCK = 128
TOK_DEV = 256
INNER = 3584
CONV = 3840
LENGTH = 16384
BATCH = 4


def draw_token_ids(key, part):
    blocks = LENGTH // TOK_DEV
    keys = jax.random.split(jax.random.fold_in(key, 3), 4)
    favoured = jax.random.randint(keys[0], (BATCH, blocks, 2), 0, VOCAB)
    which = jax.random.randint(keys[1], (BATCH, blocks, TOK_DEV), 0, 2)
    picks = jnp.take_along_axis(favoured, which, axis=2)
    spread = jax.random.randint(keys[2], (BATCH, blocks, TOK_DEV), 0, VOCAB)
    coin = jax.random.randint(keys[3], (BATCH, blocks, TOK_DEV), 0, 4)
    return jnp.where(coin == 0, spread, picks).reshape(BATCH, LENGTH).astype(jnp.int32)


def draw_decay_log(key, part):
    keys = jax.random.split(jax.random.fold_in(key, 11), 4)
    share = 0.5
    chosen = jax.random.randint(keys[3], (), 0, HEADS)
    slow = (jax.random.uniform(keys[0], (HEADS,), jnp.float32) < share) | (jnp.arange(HEADS) == chosen)
    slow_rate = jnp.exp(jax.random.uniform(keys[1], (HEADS,), jnp.float32, math.log(0.2), math.log(0.6))) / (0.07 * LENGTH)
    fast_rate = jnp.exp(jax.random.uniform(keys[2], (HEADS,), jnp.float32, math.log(1.0 / 50.0), math.log(1.0 / 30.0))) / 0.07
    return jnp.log(jnp.where(slow, slow_rate, fast_rate)).astype(jnp.float32)


def draw_cotangent(key, part):
    keys = jax.random.split(jax.random.fold_in(key, 5), 1)
    noise = jnp.clip(jax.random.normal(keys[0], (BATCH, LENGTH, INNER), jnp.float32), -4.0, 4.0)
    ramp = 1.0 + 2.0 * jnp.arange(LENGTH, dtype=jnp.float32) / LENGTH
    scale = 1.0 / math.sqrt(BATCH * LENGTH)
    result = noise * ramp[None, :, None]
    return (result * scale).astype(jnp.bfloat16)


def gaussian(key, shape, deviation, limit, kind=jnp.bfloat16):
    values = deviation * jax.random.normal(key, shape, jnp.float32)
    return jnp.clip(values, min=-limit, max=limit).astype(kind)


def setup_inputs(seed: int = 0) -> dict:
    arg_keys = jax.random.split(jax.random.key(seed), 11)
    return {
        "token_ids": draw_token_ids(jax.random.fold_in(arg_keys[10], 71), 0),
        "input_table": gaussian(arg_keys[1], (VOCAB, CONV), 1.0, 6.0),
        "gate_table": gaussian(arg_keys[2], (VOCAB, INNER), 1.0, 6.0),
        "step_table": jnp.clip(jax.random.uniform(arg_keys[3], (VOCAB, HEADS), jnp.float32, -4.5, -1.5), -4.5, -1.5),
        "decay_log": draw_decay_log(jax.random.fold_in(arg_keys[10], 71), 0),
        "conv_weight": gaussian(arg_keys[5], (CONV_WIDTH, CONV), CONV_WIDTH ** -0.5, 3.0, jnp.float32),
        "conv_bias": gaussian(arg_keys[6], (CONV,), 0.5, 3.0, jnp.float32),
        "skip_gain": jnp.clip(1.0 + 0.15 * jax.random.normal(arg_keys[7], (HEADS,), jnp.float32), 0.25, 1.75),
        "norm_gain": jnp.clip(1.0 + 0.1 * jax.random.normal(arg_keys[8], (INNER,), jnp.float32), 0.5, 1.5),
        "cotangent": draw_cotangent(jax.random.fold_in(arg_keys[10], 71), 0),
    }


EPS = 1e-05
HIGH = lax.Precision.HIGHEST

def indicator(labels, vocab):
    return (labels[:, None] == jnp.arange(vocab, dtype=jnp.int32)[None, :]).astype(jnp.float32)

def rounded(value):
    return lax.optimization_barrier(value.astype(jnp.bfloat16))

def group_step(carried, item):
    values, write_keys, read_keys, steps, log_decay = item
    cum = jnp.cumsum(log_decay, axis=0)
    last = cum[-1]
    reads = read_keys.astype(jnp.float32)
    writes = write_keys.astype(jnp.float32)
    vals = values.astype(jnp.float32)
    scores = jnp.einsum('tn,sn->ts', reads, writes)
    lower = (lax.broadcasted_iota(jnp.int32, (BLOCK, BLOCK), 0) >= lax.broadcasted_iota(jnp.int32, (BLOCK, BLOCK), 1))[None]
    track = cum.T
    power = track[:, :, None] - track[:, None, :]
    fade = jnp.where(lower, jnp.exp(jnp.where(lower, power, 0.0)), 0.0)
    mixing = rounded(scores[None] * fade * steps.T[:, None, :]).astype(jnp.float32)
    within = jnp.einsum('hts,shp->thp', mixing, vals)
    held = rounded(carried).astype(jnp.float32)
    across = jnp.exp(cum)[:, :, None] * jnp.einsum('tn,hpn->thp', reads, held)
    weighted = rounded(vals * (jnp.exp(last[None, :] - cum) * steps)[:, :, None]).astype(jnp.float32)
    fresh = jnp.einsum('shp,sn->hpn', weighted, writes)
    following = jnp.exp(last)[:, None, None] * carried + fresh
    return (following, within + across)

def sequence_forward(labels, params):
    input_t, gate_t, step_t, decay_log, conv_weight, conv_bias, skip_gain, norm_gain = params
    width = conv_weight.shape[0]
    padded = jnp.concatenate([jnp.full((width - 1,), -1, jnp.int32), labels.astype(jnp.int32)])
    raw = jnp.dot(indicator(padded, VOCAB), input_t, precision=HIGH)
    own = indicator(labels.astype(jnp.int32), VOCAB)
    gate_rows = jnp.dot(own, gate_t, precision=HIGH)
    step_rows = jnp.dot(own, step_t, precision=HIGH)
    convolved = conv_bias[None, :] + conv_weight[0][None, :] * raw[0:LENGTH]
    for offset in range(1, width):
        convolved = convolved + conv_weight[offset][None, :] * raw[offset:offset + LENGTH]
    active = jax.nn.silu(convolved)
    values = rounded(active[:, :INNER]).reshape(LENGTH, HEADS, HEAD)
    write_keys = rounded(active[:, INNER:INNER + STATE])
    read_keys = rounded(active[:, INNER + STATE:])
    steps = jax.nn.softplus(step_rows)
    log_decay = -jnp.exp(decay_log)[None, :] * steps
    count = LENGTH // BLOCK
    items = (values.reshape(count, BLOCK, HEADS, HEAD), write_keys.reshape(count, BLOCK, STATE), read_keys.reshape(count, BLOCK, STATE), steps.reshape(count, BLOCK, HEADS), log_decay.reshape(count, BLOCK, HEADS))
    start = jnp.zeros((HEADS, HEAD, STATE), jnp.float32)
    _, mixed = lax.scan(jax.checkpoint(group_step), start, items)
    mixed = mixed.reshape(LENGTH, HEADS, HEAD) + skip_gain[None, :, None] * values.astype(jnp.float32)
    gated = mixed.reshape(LENGTH, INNER) * jax.nn.silu(gate_rows)
    scale = lax.rsqrt(lax.optimization_barrier(jnp.mean(gated * gated, axis=1, keepdims=True)) + EPS)
    return (gated * scale * norm_gain[None, :]).astype(jnp.bfloat16)

def reference(token_ids, input_table, gate_table, step_table, decay_log, conv_weight, conv_bias, skip_gain, norm_gain, cotangent):
    params = (input_table.astype(jnp.float32), gate_table.astype(jnp.float32), step_table, decay_log, conv_weight, conv_bias, skip_gain, norm_gain)

    def per_sequence(totals, item):
        labels, sequence_cot = item
        produced, pull = jax.vjp(partial(sequence_forward, labels), params)
        grads = pull(sequence_cot)[0]
        return (jax.tree.map(jnp.add, totals, grads), produced)
    zeros = jax.tree.map(jnp.zeros_like, params)
    grads, produced = lax.scan(per_sequence, zeros, (token_ids, cotangent))
    return (produced, grads[0], grads[1], grads[2], grads[3], grads[4], grads[5], grads[6], grads[7])
```

```python
from functools import partial

import jax
import jax.numpy as jnp
from jax import lax
from jax.sharding import PartitionSpec as P

BLOCK = 128


EPS = 1e-05
HIGH = lax.Precision.HIGHEST


def shifted(value, axis, steps):
    count = lax.axis_size(axis)
    leading, last = (max(0, -steps), min(count, count - steps))
    return lax.ppermute(value, axis, [(source, source + steps) for source in range(leading, last)])


def indicator(labels, vocab, kind):
    return (labels[:, None] == jnp.arange(vocab, dtype=jnp.int32)[None, :]).astype(kind)


def prepare(raw_rows, step_rows, decay_log, conv_weight, conv_bias, inner, heads):
    width = conv_weight.shape[0]
    tokens = raw_rows.shape[0] - width + 1
    state = (raw_rows.shape[1] - inner) // 2
    convolved = conv_bias[None, :] + conv_weight[0][None, :] * raw_rows[0:tokens]
    for offset in range(1, width):
        convolved = convolved + conv_weight[offset][None, :] * raw_rows[offset : offset + tokens]
    active = jax.nn.silu(convolved)
    values = active[:, :inner].astype(jnp.bfloat16).reshape(tokens, heads, inner // heads)
    write_keys = active[:, inner : inner + state].astype(jnp.bfloat16)
    read_keys = active[:, inner + state :].astype(jnp.bfloat16)
    steps = jax.nn.softplus(step_rows)
    log_decay = -jnp.exp(decay_log)[None, :] * steps
    return (values, write_keys, read_keys, steps, log_decay)


def group_states(values, write_keys, steps, log_decay):
    tokens, heads, head = values.shape
    count = tokens // BLOCK
    cum = jnp.cumsum(log_decay.reshape(count, BLOCK, heads), axis=1)
    factor = jnp.exp(cum[:, -1:, :] - cum) * steps.reshape(count, BLOCK, heads)
    weighted = (values.reshape(count, BLOCK, heads, head) * factor[..., None]).astype(jnp.bfloat16)
    return jnp.einsum(
        "cshp,csn->chpn",
        weighted,
        write_keys.reshape(count, BLOCK, -1),
        preferred_element_type=jnp.float32,
    )


def local_states(pieces, log_decay):
    count = pieces.shape[0]
    block_total = jnp.sum(log_decay.reshape(count, BLOCK, -1), axis=1)

    def advance(carried, item):
        piece, total = item
        return (jnp.exp(total)[:, None, None] * carried + piece, carried)

    final, entering = lax.scan(advance, jnp.zeros_like(pieces[0]), (pieces, block_total))
    return (entering, final, jnp.sum(block_total, axis=0))


def mixer_output(
    values,
    write_keys,
    read_keys,
    steps,
    log_decay,
    entering,
    carried,
    gate_rows,
    skip_gain,
    norm_gain,
):
    tokens, heads, head = values.shape
    count = tokens // BLOCK
    cum = jnp.cumsum(log_decay.reshape(count, BLOCK, heads), axis=1)
    block_total = cum[:, -1, :]
    before = jnp.cumsum(block_total, axis=0) - block_total
    states = entering + jnp.exp(before)[:, :, None, None] * carried[None]
    writes = write_keys.reshape(count, BLOCK, -1)
    reads = read_keys.reshape(count, BLOCK, -1)
    scores = jnp.einsum("ctn,csn->cts", reads, writes, preferred_element_type=jnp.float32)
    lower = (
        lax.broadcasted_iota(jnp.int32, (BLOCK, BLOCK), 0)
        >= lax.broadcasted_iota(jnp.int32, (BLOCK, BLOCK), 1)
    )[None, None]
    track = jnp.transpose(cum, (0, 2, 1))
    power = track[:, :, :, None] - track[:, :, None, :]
    fade = jnp.where(lower, jnp.exp(jnp.where(lower, power, 0.0)), 0.0)
    widths = jnp.transpose(steps.reshape(count, BLOCK, heads), (0, 2, 1))
    mixing = (scores[:, None] * fade * widths[:, :, None, :]).astype(jnp.bfloat16)
    blocked = values.reshape(count, BLOCK, heads, head)
    within = jnp.einsum("chts,cshp->cthp", mixing, blocked, preferred_element_type=jnp.float32)
    across = jnp.exp(cum)[..., None] * jnp.einsum(
        "ctn,chpn->cthp", reads, states.astype(jnp.bfloat16), preferred_element_type=jnp.float32
    )
    mixed = within + across + skip_gain[None, None, :, None] * blocked
    gated = mixed.reshape(tokens, heads * head) * jax.nn.silu(gate_rows)
    scale = lax.rsqrt(jnp.mean(gated * gated, axis=1, keepdims=True) + EPS)
    return (gated * scale * norm_gain[None, :]).astype(jnp.bfloat16)


def carry_weights(logs, backward):
    parts = logs.shape[1]
    inclusive = jnp.cumsum(logs, axis=1)
    exclusive = inclusive - logs
    rows = lax.broadcasted_iota(jnp.int32, (parts, parts), 0)
    cols = lax.broadcasted_iota(jnp.int32, (parts, parts), 1)
    if backward:
        keep = (cols > rows)[None]
        power = exclusive[:, None, :] - inclusive[:, :, None]
    else:
        keep = (cols < rows)[None]
        power = exclusive[:, :, None] - inclusive[:, None, :]
    return jnp.where(keep, jnp.exp(jnp.where(keep, power, 0.0)), 0.0)


def settle_forward(pieces):
    states_in, totals_in = pieces
    weights = carry_weights(totals_in[:, :, 0], False)
    settled = jnp.einsum("hij,hjw->hiw", weights, states_in, precision=HIGH)
    return lax.all_to_all(settled, "seq", split_axis=1, concat_axis=1, tiled=True)


def settle_backward(pieces):
    states_in, totals_in = pieces
    weights = carry_weights(totals_in[:, :, 0], True)
    settled = jnp.einsum("hij,hjw->hiw", weights, states_in, precision=HIGH)
    return lax.all_to_all(settled, "seq", split_axis=1, concat_axis=1, tiled=True)


def local(
    token_ids,
    input_table,
    gate_table,
    step_table,
    decay_log,
    conv_weight,
    conv_bias,
    skip_gain,
    norm_gain,
    cotangent,
):
    labels = token_ids[0]
    tokens = labels.shape[0]
    width = conv_weight.shape[0]
    vocab = input_table.shape[0]
    inner = gate_table.shape[1]
    heads = step_table.shape[1]
    rim = shifted(labels[tokens - width + 1 :] + 1, "seq", 1) - 1
    extended = jnp.concatenate([rim, labels])
    wide_hot = indicator(extended, vocab, jnp.bfloat16)
    own_hot = wide_hot[width - 1 :]
    raw_rows = jnp.dot(wide_hot, input_table, preferred_element_type=jnp.float32)
    gate_rows = jnp.dot(own_hot, gate_table, preferred_element_type=jnp.float32)
    step_rows = jnp.dot(own_hot.astype(jnp.float32), step_table, precision=HIGH)
    features, pull_prepare = jax.vjp(
        partial(prepare, inner=inner, heads=heads),
        raw_rows,
        step_rows,
        decay_log,
        conv_weight,
        conv_bias,
    )
    values, write_keys, read_keys, steps, log_decay = features
    pieces, pull_groups = jax.vjp(group_states, values, write_keys, steps, log_decay)
    (entering, final, total), pull_local = jax.vjp(local_states, pieces, log_decay)
    flat = final.reshape(heads, -1)
    parts = lax.axis_size("seq")
    span = flat.shape[1] // parts
    totals = jnp.broadcast_to(total[:, None, None], (heads, parts, 1))
    carried = settle_forward(
        (
            lax.all_to_all(
                flat.reshape(heads, parts, span), "seq", split_axis=1, concat_axis=1, tiled=True
            ),
            lax.all_to_all(totals, "seq", split_axis=1, concat_axis=1, tiled=True),
        )
    )
    layer_out, pull_out = jax.vjp(
        mixer_output,
        values,
        write_keys,
        read_keys,
        steps,
        log_decay,
        entering,
        carried,
        gate_rows,
        skip_gain,
        norm_gain,
    )
    d_values, d_write, d_read, d_steps, d_log, d_entering, d_carried, d_gate, d_skip, d_norm = (
        pull_out(cotangent[0])
    )
    back_flat = d_carried.reshape(heads, -1)
    later = settle_backward(
        (
            lax.all_to_all(
                back_flat.reshape(heads, parts, span),
                "seq",
                split_axis=1,
                concat_axis=1,
                tiled=True,
            ),
            lax.all_to_all(totals, "seq", split_axis=1, concat_axis=1, tiled=True),
        )
    )
    d_total = jnp.exp(total) * jnp.sum(later * carried, axis=(1, 2))
    d_pieces, d_log_local = pull_local((d_entering, later, d_total))
    d_values_state, d_write_state, d_steps_state, d_log_state = pull_groups(d_pieces)
    d_raw, d_step_rows, d_decay, d_taps, d_shift = pull_prepare(
        (
            d_values + d_values_state,
            d_write + d_write_state,
            d_read,
            d_steps + d_steps_state,
            d_log + d_log_state + d_log_local,
        )
    )
    wide_float = wide_hot.astype(jnp.float32)
    own_float = wide_float[width - 1 :]
    parts_list = (
        jnp.dot(wide_float.T, d_raw, precision=HIGH),
        jnp.dot(own_float.T, d_gate, precision=HIGH),
        jnp.dot(own_float.T, d_step_rows, precision=HIGH),
        d_decay,
        d_taps,
        d_shift,
        d_skip,
        d_norm,
    )
    packed = jnp.concatenate([part.reshape(-1) for part in parts_list])
    packed = lax.psum(packed, ("seq", "batch"))
    sums = []
    offset = 0
    for part in parts_list:
        sums.append(packed[offset : offset + part.size].reshape(part.shape))
        offset += part.size
    return (layer_out[None], sums[0], sums[1], sums[2], sums[3], sums[4], sums[5], sums[6], sums[7])


def solution(mesh):
    return jax.shard_map(
        local,
        mesh=mesh,
        in_specs=(
            P("batch", "seq"),
            P(),
            P(),
            P(),
            P(),
            P(),
            P(),
            P(),
            P(),
            P("batch", "seq", None),
        ),
        out_specs=(P("batch", "seq", None), P(), P(), P(), P(), P(), P(), P(), P()),
        check_vma=False,
    )
```

```python
from functools import partial

import jax
import jax.numpy as jnp
from jax import lax
from jax.sharding import PartitionSpec as P

BLOCK = 128


EPS = 1e-05
HIGH = lax.Precision.HIGHEST


def shifted(value, axis, steps):
    count = lax.axis_size(axis)
    leading, last = (max(0, -steps), min(count, count - steps))
    return lax.ppermute(value, axis, [(source, source + steps) for source in range(leading, last)])


def indicator(labels, vocab, kind):
    return (labels[:, None] == jnp.arange(vocab, dtype=jnp.int32)[None, :]).astype(kind)


def prepare(raw_rows, step_rows, decay_log, conv_weight, conv_bias, inner, heads):
    width = conv_weight.shape[0]
    tokens = raw_rows.shape[0] - width + 1
    state = (raw_rows.shape[1] - inner) // 2
    convolved = conv_bias[None, :] + conv_weight[0][None, :] * raw_rows[0:tokens]
    for offset in range(1, width):
        convolved = convolved + conv_weight[offset][None, :] * raw_rows[offset : offset + tokens]
    active = jax.nn.silu(convolved)
    values = active[:, :inner].astype(jnp.bfloat16).reshape(tokens, heads, inner // heads)
    write_keys = active[:, inner : inner + state].astype(jnp.bfloat16)
    read_keys = active[:, inner + state :].astype(jnp.bfloat16)
    steps = jax.nn.softplus(step_rows)
    log_decay = -jnp.exp(decay_log)[None, :] * steps
    return (values, write_keys, read_keys, steps, log_decay)


def group_states(values, write_keys, steps, log_decay):
    tokens, heads, head = values.shape
    count = tokens // BLOCK
    cum = jnp.cumsum(log_decay.reshape(count, BLOCK, heads), axis=1)
    factor = jnp.exp(cum[:, -1:, :] - cum) * steps.reshape(count, BLOCK, heads)
    weighted = (values.reshape(count, BLOCK, heads, head) * factor[..., None]).astype(jnp.bfloat16)
    return jnp.einsum(
        "cshp,csn->chpn",
        weighted,
        write_keys.reshape(count, BLOCK, -1),
        preferred_element_type=jnp.float32,
    )


def local_states(pieces, log_decay):
    count = pieces.shape[0]
    block_total = jnp.sum(log_decay.reshape(count, BLOCK, -1), axis=1)

    def advance(carried, item):
        piece, total = item
        return (jnp.exp(total)[:, None, None] * carried + piece, carried)

    final, entering = lax.scan(advance, jnp.zeros_like(pieces[0]), (pieces, block_total))
    return (entering, final, jnp.sum(block_total, axis=0))


def mixer_output(
    values,
    write_keys,
    read_keys,
    steps,
    log_decay,
    entering,
    carried,
    gate_rows,
    skip_gain,
    norm_gain,
):
    tokens, heads, head = values.shape
    count = tokens // BLOCK
    cum = jnp.cumsum(log_decay.reshape(count, BLOCK, heads), axis=1)
    block_total = cum[:, -1, :]
    before = jnp.cumsum(block_total, axis=0) - block_total
    states = entering + jnp.exp(before)[:, :, None, None] * carried[None]
    writes = write_keys.reshape(count, BLOCK, -1)
    reads = read_keys.reshape(count, BLOCK, -1)
    scores = jnp.einsum("ctn,csn->cts", reads, writes, preferred_element_type=jnp.float32)
    lower = (
        lax.broadcasted_iota(jnp.int32, (BLOCK, BLOCK), 0)
        >= lax.broadcasted_iota(jnp.int32, (BLOCK, BLOCK), 1)
    )[None, None]
    track = jnp.transpose(cum, (0, 2, 1))
    power = track[:, :, :, None] - track[:, :, None, :]
    fade = jnp.where(lower, jnp.exp(jnp.where(lower, power, 0.0)), 0.0)
    widths = jnp.transpose(steps.reshape(count, BLOCK, heads), (0, 2, 1))
    mixing = (scores[:, None] * fade * widths[:, :, None, :]).astype(jnp.bfloat16)
    blocked = values.reshape(count, BLOCK, heads, head)
    within = jnp.einsum("chts,cshp->cthp", mixing, blocked, preferred_element_type=jnp.float32)
    across = jnp.exp(cum)[..., None] * jnp.einsum(
        "ctn,chpn->cthp", reads, states.astype(jnp.bfloat16), preferred_element_type=jnp.float32
    )
    mixed = within + across + skip_gain[None, None, :, None] * blocked
    gated = mixed.reshape(tokens, heads * head) * jax.nn.silu(gate_rows)
    scale = lax.rsqrt(jnp.mean(gated * gated, axis=1, keepdims=True) + EPS)
    return (gated * scale * norm_gain[None, :]).astype(jnp.bfloat16)


def carry_weights(logs, backward):
    parts = logs.shape[1]
    inclusive = jnp.cumsum(logs, axis=1)
    exclusive = inclusive - logs
    rows = lax.broadcasted_iota(jnp.int32, (parts, parts), 0)
    cols = lax.broadcasted_iota(jnp.int32, (parts, parts), 1)
    if backward:
        keep = (cols > rows)[None]
        power = exclusive[:, None, :] - inclusive[:, :, None]
    else:
        keep = (cols < rows)[None]
        power = exclusive[:, :, None] - inclusive[:, None, :]
    return jnp.where(keep, jnp.exp(jnp.where(keep, power, 0.0)), 0.0)


def settle_forward(pieces):
    states_in, totals_in = pieces
    weights = carry_weights(totals_in[:, :, 0], False)
    settled = jnp.einsum("hij,hjw->hiw", weights, states_in, precision=HIGH)
    return lax.all_to_all(settled, "seq", split_axis=1, concat_axis=1, tiled=True)


def settle_backward(pieces):
    states_in, totals_in = pieces
    weights = carry_weights(totals_in[:, :, 0], True)
    settled = jnp.einsum("hij,hjw->hiw", weights, states_in, precision=HIGH)
    return lax.all_to_all(settled, "seq", split_axis=1, concat_axis=1, tiled=True)


def spread_sum(flat, axes):
    count = 1
    for axis in axes:
        count *= lax.axis_size(axis)
    size = flat.shape[0]
    chunk = -(-size // count)
    padded = jnp.pad(flat, (0, chunk * count - size)).reshape(count, chunk)
    gathered = lax.all_to_all(padded, axes, split_axis=0, concat_axis=0, tiled=True)
    reduced = jnp.sum(gathered, axis=0, keepdims=True)
    spread = jnp.broadcast_to(reduced, (count, chunk))
    whole = lax.all_to_all(spread, axes, split_axis=0, concat_axis=0, tiled=True)
    return whole.reshape(-1)[:size]


def local(
    token_ids,
    input_table,
    gate_table,
    step_table,
    decay_log,
    conv_weight,
    conv_bias,
    skip_gain,
    norm_gain,
    cotangent,
):
    labels = token_ids[0]
    tokens = labels.shape[0]
    width = conv_weight.shape[0]
    vocab = input_table.shape[0]
    inner = gate_table.shape[1]
    heads = step_table.shape[1]
    rim = shifted(labels[tokens - width + 1 :] + 1, "seq", 1) - 1
    extended = jnp.concatenate([rim, labels])
    wide_hot = indicator(extended, vocab, jnp.bfloat16)
    own_hot = wide_hot[width - 1 :]
    raw_rows = jnp.dot(wide_hot, input_table, preferred_element_type=jnp.float32)
    gate_rows = jnp.dot(own_hot, gate_table, preferred_element_type=jnp.float32)
    step_rows = jnp.dot(own_hot.astype(jnp.float32), step_table, precision=HIGH)
    features, pull_prepare = jax.vjp(
        partial(prepare, inner=inner, heads=heads),
        raw_rows,
        step_rows,
        decay_log,
        conv_weight,
        conv_bias,
    )
    values, write_keys, read_keys, steps, log_decay = features
    pieces, pull_groups = jax.vjp(group_states, values, write_keys, steps, log_decay)
    (entering, final, total), pull_local = jax.vjp(local_states, pieces, log_decay)
    flat = final.reshape(heads, -1)
    parts = lax.axis_size("seq")
    span = flat.shape[1] // parts
    totals = jnp.broadcast_to(total[:, None, None], (heads, parts, 1))
    carried = settle_forward(
        (
            lax.all_to_all(
                flat.reshape(heads, parts, span), "seq", split_axis=1, concat_axis=1, tiled=True
            ),
            lax.all_to_all(totals, "seq", split_axis=1, concat_axis=1, tiled=True),
        )
    )
    layer_out, pull_out = jax.vjp(
        mixer_output,
        values,
        write_keys,
        read_keys,
        steps,
        log_decay,
        entering,
        carried,
        gate_rows,
        skip_gain,
        norm_gain,
    )
    d_values, d_write, d_read, d_steps, d_log, d_entering, d_carried, d_gate, d_skip, d_norm = (
        pull_out(cotangent[0])
    )
    back_flat = d_carried.reshape(heads, -1)
    later = settle_backward(
        (
            lax.all_to_all(
                back_flat.reshape(heads, parts, span),
                "seq",
                split_axis=1,
                concat_axis=1,
                tiled=True,
            ),
            lax.all_to_all(totals, "seq", split_axis=1, concat_axis=1, tiled=True),
        )
    )
    d_total = jnp.exp(total) * jnp.sum(later * carried, axis=(1, 2))
    d_pieces, d_log_local = pull_local((d_entering, later, d_total))
    d_values_state, d_write_state, d_steps_state, d_log_state = pull_groups(d_pieces)
    d_raw, d_step_rows, d_decay, d_taps, d_shift = pull_prepare(
        (
            d_values + d_values_state,
            d_write + d_write_state,
            d_read,
            d_steps + d_steps_state,
            d_log + d_log_state + d_log_local,
        )
    )
    wide_float = wide_hot.astype(jnp.float32)
    own_float = wide_float[width - 1 :]
    parts_list = (
        jnp.dot(wide_float.T, d_raw, precision=HIGH),
        jnp.dot(own_float.T, d_gate, precision=HIGH),
        jnp.dot(own_float.T, d_step_rows, precision=HIGH),
        d_decay,
        d_taps,
        d_shift,
        d_skip,
        d_norm,
    )
    packed = jnp.concatenate([part.reshape(-1) for part in parts_list])
    packed = spread_sum(packed, ("seq", "batch"))
    sums = []
    offset = 0
    for part in parts_list:
        sums.append(packed[offset : offset + part.size].reshape(part.shape))
        offset += part.size
    return (layer_out[None], sums[0], sums[1], sums[2], sums[3], sums[4], sums[5], sums[6], sums[7])


def solution(mesh):
    return jax.shard_map(
        local,
        mesh=mesh,
        in_specs=(
            P("batch", "seq"),
            P(),
            P(),
            P(),
            P(),
            P(),
            P(),
            P(),
            P(),
            P("batch", "seq", None),
        ),
        out_specs=(P("batch", "seq", None), P(), P(), P(), P(), P(), P(), P(), P()),
        check_vma=False,
    )
```

```python
from functools import partial

import jax
import jax.numpy as jnp
from jax import lax
from jax.sharding import PartitionSpec as P

BLOCK = 128


EPS = 1e-05
HIGH = lax.Precision.HIGHEST


def shifted(value, axis, steps):
    count = lax.axis_size(axis)
    leading, last = (max(0, -steps), min(count, count - steps))
    return lax.ppermute(value, axis, [(source, source + steps) for source in range(leading, last)])


def indicator(labels, vocab, kind):
    return (labels[:, None] == jnp.arange(vocab, dtype=jnp.int32)[None, :]).astype(kind)


def prepare(raw_rows, step_rows, decay_log, conv_weight, conv_bias, inner, heads):
    width = conv_weight.shape[0]
    tokens = raw_rows.shape[0] - width + 1
    state = (raw_rows.shape[1] - inner) // 2
    convolved = conv_bias[None, :] + conv_weight[0][None, :] * raw_rows[0:tokens]
    for offset in range(1, width):
        convolved = convolved + conv_weight[offset][None, :] * raw_rows[offset : offset + tokens]
    active = jax.nn.silu(convolved)
    values = active[:, :inner].astype(jnp.bfloat16).reshape(tokens, heads, inner // heads)
    write_keys = active[:, inner : inner + state].astype(jnp.bfloat16)
    read_keys = active[:, inner + state :].astype(jnp.bfloat16)
    steps = jax.nn.softplus(step_rows)
    log_decay = -jnp.exp(decay_log)[None, :] * steps
    return (values, write_keys, read_keys, steps, log_decay)


def group_states(values, write_keys, steps, log_decay):
    tokens, heads, head = values.shape
    count = tokens // BLOCK
    cum = jnp.cumsum(log_decay.reshape(count, BLOCK, heads), axis=1)
    factor = jnp.exp(cum[:, -1:, :] - cum) * steps.reshape(count, BLOCK, heads)
    weighted = (values.reshape(count, BLOCK, heads, head) * factor[..., None]).astype(jnp.bfloat16)
    return jnp.einsum(
        "cshp,csn->chpn",
        weighted,
        write_keys.reshape(count, BLOCK, -1),
        preferred_element_type=jnp.float32,
    )


def local_states(pieces, log_decay):
    count = pieces.shape[0]
    block_total = jnp.sum(log_decay.reshape(count, BLOCK, -1), axis=1)

    def advance(carried, item):
        piece, total = item
        return (jnp.exp(total)[:, None, None] * carried + piece, carried)

    final, entering = lax.scan(
        advance, jnp.zeros_like(pieces[0]), (pieces, block_total), unroll=True
    )
    return (entering, final, jnp.sum(block_total, axis=0))


def mixer_output(
    values,
    write_keys,
    read_keys,
    steps,
    log_decay,
    entering,
    carried,
    gate_rows,
    skip_gain,
    norm_gain,
):
    tokens, heads, head = values.shape
    count = tokens // BLOCK
    cum = jnp.cumsum(log_decay.reshape(count, BLOCK, heads), axis=1)
    block_total = cum[:, -1, :]
    before = jnp.cumsum(block_total, axis=0) - block_total
    states = entering + jnp.exp(before)[:, :, None, None] * carried[None]
    writes = write_keys.reshape(count, BLOCK, -1)
    reads = read_keys.reshape(count, BLOCK, -1)
    scores = jnp.einsum("ctn,csn->cts", reads, writes, preferred_element_type=jnp.float32)
    lower = (
        lax.broadcasted_iota(jnp.int32, (BLOCK, BLOCK), 0)
        >= lax.broadcasted_iota(jnp.int32, (BLOCK, BLOCK), 1)
    )[None, None]
    track = jnp.transpose(cum, (0, 2, 1))
    power = track[:, :, :, None] - track[:, :, None, :]
    fade = jnp.where(lower, jnp.exp(jnp.where(lower, power, 0.0)), 0.0)
    widths = jnp.transpose(steps.reshape(count, BLOCK, heads), (0, 2, 1))
    mixing = (scores[:, None] * fade * widths[:, :, None, :]).astype(jnp.bfloat16)
    blocked = values.reshape(count, BLOCK, heads, head)
    within = jnp.einsum("chts,cshp->cthp", mixing, blocked, preferred_element_type=jnp.float32)
    across = jnp.exp(cum)[..., None] * jnp.einsum(
        "ctn,chpn->cthp", reads, states.astype(jnp.bfloat16), preferred_element_type=jnp.float32
    )
    mixed = within + across + skip_gain[None, None, :, None] * blocked
    gated = mixed.reshape(tokens, heads * head) * jax.nn.silu(gate_rows)
    scale = lax.rsqrt(jnp.mean(gated * gated, axis=1, keepdims=True) + EPS)
    return (gated * scale * norm_gain[None, :]).astype(jnp.bfloat16)


def carry_weights(logs, backward):
    parts = logs.shape[1]
    inclusive = jnp.cumsum(logs, axis=1)
    exclusive = inclusive - logs
    rows = lax.broadcasted_iota(jnp.int32, (parts, parts), 0)
    cols = lax.broadcasted_iota(jnp.int32, (parts, parts), 1)
    if backward:
        keep = (cols > rows)[None]
        power = exclusive[:, None, :] - inclusive[:, :, None]
    else:
        keep = (cols < rows)[None]
        power = exclusive[:, :, None] - inclusive[:, None, :]
    return jnp.where(keep, jnp.exp(jnp.where(keep, power, 0.0)), 0.0)


def settle_forward(pieces):
    states_in, totals_in = pieces
    weights = carry_weights(totals_in[:, :, 0], False)
    settled = jnp.einsum("hij,hjw->hiw", weights, states_in, precision=HIGH)
    return lax.all_to_all(settled, "seq", split_axis=1, concat_axis=1, tiled=True)


def settle_backward(pieces):
    states_in, totals_in = pieces
    weights = carry_weights(totals_in[:, :, 0], True)
    settled = jnp.einsum("hij,hjw->hiw", weights, states_in, precision=HIGH)
    return lax.all_to_all(settled, "seq", split_axis=1, concat_axis=1, tiled=True)


def spread_sum(flat, axes):
    count = 1
    for axis in axes:
        count *= lax.axis_size(axis)
    size = flat.shape[0]
    chunk = -(-size // count)
    padded = jnp.pad(flat, (0, chunk * count - size)).reshape(count, chunk)
    gathered = lax.all_to_all(padded, axes, split_axis=0, concat_axis=0, tiled=True)
    reduced = jnp.sum(gathered, axis=0, keepdims=True)
    spread = jnp.broadcast_to(reduced, (count, chunk))
    whole = lax.all_to_all(spread, axes, split_axis=0, concat_axis=0, tiled=True)
    return whole.reshape(-1)[:size]


def local(
    token_ids,
    input_table,
    gate_table,
    step_table,
    decay_log,
    conv_weight,
    conv_bias,
    skip_gain,
    norm_gain,
    cotangent,
):
    labels = token_ids[0]
    tokens = labels.shape[0]
    width = conv_weight.shape[0]
    vocab = input_table.shape[0]
    inner = gate_table.shape[1]
    heads = step_table.shape[1]
    rim = shifted(labels[tokens - width + 1 :] + 1, "seq", 1) - 1
    extended = jnp.concatenate([rim, labels])
    wide_hot = indicator(extended, vocab, jnp.bfloat16)
    own_hot = wide_hot[width - 1 :]
    raw_rows = jnp.dot(wide_hot, input_table, preferred_element_type=jnp.float32)
    gate_rows = jnp.dot(own_hot, gate_table, preferred_element_type=jnp.float32)
    step_rows = jnp.dot(own_hot.astype(jnp.float32), step_table, precision=HIGH)
    features, pull_prepare = jax.vjp(
        partial(prepare, inner=inner, heads=heads),
        raw_rows,
        step_rows,
        decay_log,
        conv_weight,
        conv_bias,
    )
    values, write_keys, read_keys, steps, log_decay = features
    pieces, pull_groups = jax.vjp(group_states, values, write_keys, steps, log_decay)
    (entering, final, total), pull_local = jax.vjp(local_states, pieces, log_decay)
    flat = final.reshape(heads, -1)
    parts = lax.axis_size("seq")
    span = flat.shape[1] // parts
    total_row = jnp.zeros((1, parts, span), jnp.float32).at[0, :, :heads].set(
        jnp.broadcast_to(total[None, :], (parts, heads))
    )
    outgoing = jnp.concatenate([flat.reshape(heads, parts, span), total_row], axis=0)
    incoming = lax.all_to_all(outgoing, "seq", split_axis=1, concat_axis=1, tiled=True)
    totals = jnp.transpose(incoming[heads, :, :heads])[:, :, None]
    carried = settle_forward((incoming[:heads], totals))
    layer_out, pull_out = jax.vjp(
        mixer_output,
        values,
        write_keys,
        read_keys,
        steps,
        log_decay,
        entering,
        carried,
        gate_rows,
        skip_gain,
        norm_gain,
    )
    d_values, d_write, d_read, d_steps, d_log, d_entering, d_carried, d_gate, d_skip, d_norm = (
        pull_out(cotangent[0])
    )
    back_flat = d_carried.reshape(heads, -1)
    later = settle_backward(
        (
            lax.all_to_all(
                back_flat.reshape(heads, parts, span),
                "seq",
                split_axis=1,
                concat_axis=1,
                tiled=True,
            ),
            totals,
        )
    )
    d_total = jnp.exp(total) * jnp.sum(later * carried, axis=(1, 2))
    d_pieces, d_log_local = pull_local((d_entering, later, d_total))
    d_values_state, d_write_state, d_steps_state, d_log_state = pull_groups(d_pieces)
    d_raw, d_step_rows, d_decay, d_taps, d_shift = pull_prepare(
        (
            d_values + d_values_state,
            d_write + d_write_state,
            d_read,
            d_steps + d_steps_state,
            d_log + d_log_state + d_log_local,
        )
    )
    wide_float = wide_hot.astype(jnp.float32)
    own_float = wide_float[width - 1 :]
    parts_list = (
        jnp.dot(wide_float.T, d_raw, precision=HIGH),
        jnp.dot(own_float.T, d_gate, precision=HIGH),
        jnp.dot(own_float.T, d_step_rows, precision=HIGH),
        d_decay,
        d_taps,
        d_shift,
        d_skip,
        d_norm,
    )
    packed = jnp.concatenate([part.reshape(-1) for part in parts_list])
    packed = spread_sum(packed, ("seq", "batch"))
    sums = []
    offset = 0
    for part in parts_list:
        sums.append(packed[offset : offset + part.size].reshape(part.shape))
        offset += part.size
    return (layer_out[None], sums[0], sums[1], sums[2], sums[3], sums[4], sums[5], sums[6], sums[7])


def solution(mesh):
    return jax.shard_map(
        local,
        mesh=mesh,
        in_specs=(
            P("batch", "seq"),
            P(),
            P(),
            P(),
            P(),
            P(),
            P(),
            P(),
            P(),
            P("batch", "seq", None),
        ),
        out_specs=(P("batch", "seq", None), P(), P(), P(), P(), P(), P(), P(), P()),
        check_vma=False,
    )
```

```python
from functools import partial

import jax
import jax.numpy as jnp
from jax import lax
from jax.sharding import PartitionSpec as P

BLOCK = 128


EPS = 1e-05
HIGH = lax.Precision.HIGHEST


def shifted(value, axis, steps):
    count = lax.axis_size(axis)
    leading, last = (max(0, -steps), min(count, count - steps))
    return lax.ppermute(value, axis, [(source, source + steps) for source in range(leading, last)])


def indicator(labels, vocab, kind):
    return (labels[:, None] == jnp.arange(vocab, dtype=jnp.int32)[None, :]).astype(kind)


def prepare(raw_rows, step_rows, decay_log, conv_weight, conv_bias, inner, heads):
    width = conv_weight.shape[0]
    tokens = raw_rows.shape[0] - width + 1
    state = (raw_rows.shape[1] - inner) // 2
    convolved = conv_bias[None, :] + conv_weight[0][None, :] * raw_rows[0:tokens]
    for offset in range(1, width):
        convolved = convolved + conv_weight[offset][None, :] * raw_rows[offset : offset + tokens]
    active = jax.nn.silu(convolved)
    values = active[:, :inner].astype(jnp.bfloat16).reshape(tokens, heads, inner // heads)
    write_keys = active[:, inner : inner + state].astype(jnp.bfloat16)
    read_keys = active[:, inner + state :].astype(jnp.bfloat16)
    steps = jax.nn.softplus(step_rows)
    log_decay = -jnp.exp(decay_log)[None, :] * steps
    return (values, write_keys, read_keys, steps, log_decay)


def group_states(values, write_keys, steps, log_decay):
    tokens, heads, head = values.shape
    count = tokens // BLOCK
    cum = jnp.cumsum(log_decay.reshape(count, BLOCK, heads), axis=1)
    factor = jnp.exp(cum[:, -1:, :] - cum) * steps.reshape(count, BLOCK, heads)
    weighted = (values.reshape(count, BLOCK, heads, head) * factor[..., None]).astype(jnp.bfloat16)
    return jnp.einsum(
        "cshp,csn->chpn",
        weighted,
        write_keys.reshape(count, BLOCK, -1),
        preferred_element_type=jnp.float32,
    )


def local_states(pieces, log_decay):
    count = pieces.shape[0]
    block_total = jnp.sum(log_decay.reshape(count, BLOCK, -1), axis=1)

    def advance(carried, item):
        piece, total = item
        return (jnp.exp(total)[:, None, None] * carried + piece, carried)

    final, entering = lax.scan(
        advance, jnp.zeros_like(pieces[0]), (pieces, block_total), unroll=True
    )
    return (entering, final, jnp.sum(block_total, axis=0))


def intra(values, write_keys, read_keys, steps, log_decay):
    tokens, heads, head = values.shape
    count = tokens // BLOCK
    cum = jnp.cumsum(log_decay.reshape(count, BLOCK, heads), axis=1)
    writes = write_keys.reshape(count, BLOCK, -1)
    reads = read_keys.reshape(count, BLOCK, -1)
    scores = jnp.einsum("ctn,csn->cts", reads, writes, preferred_element_type=jnp.float32)
    lower = (
        lax.broadcasted_iota(jnp.int32, (BLOCK, BLOCK), 0)
        >= lax.broadcasted_iota(jnp.int32, (BLOCK, BLOCK), 1)
    )[None, None]
    track = jnp.transpose(cum, (0, 2, 1))
    power = track[:, :, :, None] - track[:, :, None, :]
    fade = jnp.where(lower, jnp.exp(jnp.where(lower, power, 0.0)), 0.0)
    widths = jnp.transpose(steps.reshape(count, BLOCK, heads), (0, 2, 1))
    mixing = (scores[:, None] * fade * widths[:, :, None, :]).astype(jnp.bfloat16)
    blocked = values.reshape(count, BLOCK, heads, head)
    return jnp.einsum("chts,cshp->cthp", mixing, blocked, preferred_element_type=jnp.float32)


def mixer_output(
    values,
    read_keys,
    log_decay,
    entering,
    carried,
    within,
    gate_rows,
    skip_gain,
    norm_gain,
):
    tokens, heads, head = values.shape
    count = tokens // BLOCK
    cum = jnp.cumsum(log_decay.reshape(count, BLOCK, heads), axis=1)
    block_total = cum[:, -1, :]
    before = jnp.cumsum(block_total, axis=0) - block_total
    states = entering + jnp.exp(before)[:, :, None, None] * carried[None]
    reads = read_keys.reshape(count, BLOCK, -1)
    blocked = values.reshape(count, BLOCK, heads, head)
    across = jnp.exp(cum)[..., None] * jnp.einsum(
        "ctn,chpn->cthp", reads, states.astype(jnp.bfloat16), preferred_element_type=jnp.float32
    )
    mixed = within + across + skip_gain[None, None, :, None] * blocked
    gated = mixed.reshape(tokens, heads * head) * jax.nn.silu(gate_rows)
    scale = lax.rsqrt(jnp.mean(gated * gated, axis=1, keepdims=True) + EPS)
    return (gated * scale * norm_gain[None, :]).astype(jnp.bfloat16)


def carry_weights(logs, backward):
    parts = logs.shape[1]
    inclusive = jnp.cumsum(logs, axis=1)
    exclusive = inclusive - logs
    rows = lax.broadcasted_iota(jnp.int32, (parts, parts), 0)
    cols = lax.broadcasted_iota(jnp.int32, (parts, parts), 1)
    if backward:
        keep = (cols > rows)[None]
        power = exclusive[:, None, :] - inclusive[:, :, None]
    else:
        keep = (cols < rows)[None]
        power = exclusive[:, :, None] - inclusive[:, None, :]
    return jnp.where(keep, jnp.exp(jnp.where(keep, power, 0.0)), 0.0)


def settle_forward(pieces):
    states_in, totals_in = pieces
    weights = carry_weights(totals_in[:, :, 0], False)
    settled = jnp.einsum("hij,hjw->hiw", weights, states_in, precision=HIGH)
    return lax.all_to_all(settled, "seq", split_axis=1, concat_axis=1, tiled=True)


def settle_backward(pieces):
    states_in, totals_in = pieces
    weights = carry_weights(totals_in[:, :, 0], True)
    settled = jnp.einsum("hij,hjw->hiw", weights, states_in, precision=HIGH)
    return lax.all_to_all(settled, "seq", split_axis=1, concat_axis=1, tiled=True)


def spread_sum(flat, axes):
    count = 1
    for axis in axes:
        count *= lax.axis_size(axis)
    size = flat.shape[0]
    chunk = -(-size // count)
    padded = jnp.pad(flat, (0, chunk * count - size)).reshape(count, chunk)
    gathered = lax.all_to_all(padded, axes, split_axis=0, concat_axis=0, tiled=True)
    reduced = jnp.sum(gathered, axis=0, keepdims=True)
    spread = jnp.broadcast_to(reduced, (count, chunk))
    whole = lax.all_to_all(spread, axes, split_axis=0, concat_axis=0, tiled=True)
    return whole.reshape(-1)[:size]


def local(
    token_ids,
    input_table,
    gate_table,
    step_table,
    decay_log,
    conv_weight,
    conv_bias,
    skip_gain,
    norm_gain,
    cotangent,
):
    labels = token_ids[0]
    tokens = labels.shape[0]
    width = conv_weight.shape[0]
    vocab = input_table.shape[0]
    inner = gate_table.shape[1]
    heads = step_table.shape[1]
    rim = shifted(labels[tokens - width + 1 :] + 1, "seq", 1) - 1
    extended = jnp.concatenate([rim, labels])
    wide_hot = indicator(extended, vocab, jnp.bfloat16)
    own_hot = wide_hot[width - 1 :]
    raw_rows = jnp.dot(wide_hot, input_table, preferred_element_type=jnp.float32)
    gate_rows = jnp.dot(own_hot, gate_table, preferred_element_type=jnp.float32)
    step_rows = jnp.dot(own_hot.astype(jnp.float32), step_table, precision=HIGH)
    features, pull_prepare = jax.vjp(
        partial(prepare, inner=inner, heads=heads),
        raw_rows,
        step_rows,
        decay_log,
        conv_weight,
        conv_bias,
    )
    values, write_keys, read_keys, steps, log_decay = features
    pieces, pull_groups = jax.vjp(group_states, values, write_keys, steps, log_decay)
    (entering, final, total), pull_local = jax.vjp(local_states, pieces, log_decay)
    flat = final.reshape(heads, -1)
    parts = lax.axis_size("seq")
    span = flat.shape[1] // parts
    total_row = jnp.zeros((1, parts, span), jnp.float32).at[0, :, :heads].set(
        jnp.broadcast_to(total[None, :], (parts, heads))
    )
    outgoing = jnp.concatenate([flat.reshape(heads, parts, span), total_row], axis=0)
    within, pull_intra = jax.vjp(intra, values, write_keys, read_keys, steps, log_decay)
    incoming = lax.all_to_all(outgoing, "seq", split_axis=1, concat_axis=1, tiled=True)
    incoming, within = lax.optimization_barrier((incoming, within))
    totals = jnp.transpose(incoming[heads, :, :heads])[:, :, None]
    carried = settle_forward((incoming[:heads], totals))
    layer_out, pull_out = jax.vjp(
        mixer_output,
        values,
        read_keys,
        log_decay,
        entering,
        carried,
        within,
        gate_rows,
        skip_gain,
        norm_gain,
    )
    d_values, d_read, d_log, d_entering, d_carried, d_within, d_gate, d_skip, d_norm = pull_out(
        cotangent[0]
    )
    back_flat = d_carried.reshape(heads, -1)
    back_incoming = lax.all_to_all(
        back_flat.reshape(heads, parts, span), "seq", split_axis=1, concat_axis=1, tiled=True
    )
    d_intra = pull_intra(d_within)
    back_incoming, d_intra = lax.optimization_barrier((back_incoming, d_intra))
    later = settle_backward((back_incoming, totals))
    d_total = jnp.exp(total) * jnp.sum(later * carried, axis=(1, 2))
    d_pieces, d_log_local = pull_local((d_entering, later, d_total))
    d_values_state, d_write_state, d_steps_state, d_log_state = pull_groups(d_pieces)
    d_raw, d_step_rows, d_decay, d_taps, d_shift = pull_prepare(
        (
            d_values + d_intra[0] + d_values_state,
            d_intra[1] + d_write_state,
            d_read + d_intra[2],
            d_intra[3] + d_steps_state,
            d_log + d_intra[4] + d_log_state + d_log_local,
        )
    )
    wide_float = wide_hot.astype(jnp.float32)
    own_float = wide_float[width - 1 :]
    parts_list = (
        jnp.dot(wide_float.T, d_raw, precision=HIGH),
        jnp.dot(own_float.T, d_gate, precision=HIGH),
        jnp.dot(own_float.T, d_step_rows, precision=HIGH),
        d_decay,
        d_taps,
        d_shift,
        d_skip,
        d_norm,
    )
    packed = jnp.concatenate([part.reshape(-1) for part in parts_list])
    packed = spread_sum(packed, ("seq", "batch"))
    sums = []
    offset = 0
    for part in parts_list:
        sums.append(packed[offset : offset + part.size].reshape(part.shape))
        offset += part.size
    return (layer_out[None], sums[0], sums[1], sums[2], sums[3], sums[4], sums[5], sums[6], sums[7])


def solution(mesh):
    return jax.shard_map(
        local,
        mesh=mesh,
        in_specs=(
            P("batch", "seq"),
            P(),
            P(),
            P(),
            P(),
            P(),
            P(),
            P(),
            P(),
            P("batch", "seq", None),
        ),
        out_specs=(P("batch", "seq", None), P(), P(), P(), P(), P(), P(), P(), P()),
        check_vma=False,
    )
```

```python
from functools import partial

import jax
import jax.numpy as jnp
from jax import lax
from jax.sharding import PartitionSpec as P

BLOCK = 128


EPS = 1e-05
HIGH = lax.Precision.HIGHEST


def shifted(value, axis, steps):
    count = lax.axis_size(axis)
    leading, last = (max(0, -steps), min(count, count - steps))
    return lax.ppermute(value, axis, [(source, source + steps) for source in range(leading, last)])


def indicator(labels, vocab, kind):
    return (labels[:, None] == jnp.arange(vocab, dtype=jnp.int32)[None, :]).astype(kind)


def prepare(raw_rows, step_rows, decay_log, conv_weight, conv_bias, inner, heads):
    width = conv_weight.shape[0]
    tokens = raw_rows.shape[0] - width + 1
    state = (raw_rows.shape[1] - inner) // 2
    convolved = conv_bias[None, :] + conv_weight[0][None, :] * raw_rows[0:tokens]
    for offset in range(1, width):
        convolved = convolved + conv_weight[offset][None, :] * raw_rows[offset : offset + tokens]
    active = jax.nn.silu(convolved)
    values = active[:, :inner].astype(jnp.bfloat16).reshape(tokens, heads, inner // heads)
    write_keys = active[:, inner : inner + state].astype(jnp.bfloat16)
    read_keys = active[:, inner + state :].astype(jnp.bfloat16)
    steps = jax.nn.softplus(step_rows)
    log_decay = -jnp.exp(decay_log)[None, :] * steps
    return (values, write_keys, read_keys, steps, log_decay)


def group_states(values, write_keys, steps, log_decay):
    tokens, heads, head = values.shape
    count = tokens // BLOCK
    cum = jnp.cumsum(log_decay.reshape(count, BLOCK, heads), axis=1)
    factor = jnp.exp(cum[:, -1:, :] - cum) * steps.reshape(count, BLOCK, heads)
    weighted = (values.reshape(count, BLOCK, heads, head) * factor[..., None]).astype(jnp.bfloat16)
    return jnp.einsum(
        "cshp,csn->chpn",
        weighted,
        write_keys.reshape(count, BLOCK, -1),
        preferred_element_type=jnp.float32,
    )


def local_states(pieces, log_decay):
    count = pieces.shape[0]
    block_total = jnp.sum(log_decay.reshape(count, BLOCK, -1), axis=1)

    def advance(carried, item):
        piece, total = item
        return (jnp.exp(total)[:, None, None] * carried + piece, carried)

    final, entering = lax.scan(
        advance, jnp.zeros_like(pieces[0]), (pieces, block_total), unroll=True
    )
    return (entering, final, jnp.sum(block_total, axis=0))


def intra(values, write_keys, read_keys, steps, log_decay):
    tokens, heads, head = values.shape
    count = tokens // BLOCK
    cum = jnp.cumsum(log_decay.reshape(count, BLOCK, heads), axis=1)
    writes = write_keys.reshape(count, BLOCK, -1)
    reads = read_keys.reshape(count, BLOCK, -1)
    scores = jnp.einsum("ctn,csn->cts", reads, writes, preferred_element_type=jnp.float32)
    lower = (
        lax.broadcasted_iota(jnp.int32, (BLOCK, BLOCK), 0)
        >= lax.broadcasted_iota(jnp.int32, (BLOCK, BLOCK), 1)
    )[None, None]
    track = jnp.transpose(cum, (0, 2, 1))
    power = track[:, :, :, None] - track[:, :, None, :]
    fade = jnp.where(lower, jnp.exp(jnp.where(lower, power, 0.0)), 0.0)
    widths = jnp.transpose(steps.reshape(count, BLOCK, heads), (0, 2, 1))
    mixing = (scores[:, None] * fade * widths[:, :, None, :]).astype(jnp.bfloat16)
    blocked = values.reshape(count, BLOCK, heads, head)
    return jnp.einsum("chts,cshp->cthp", mixing, blocked, preferred_element_type=jnp.float32)


def mixer_output(
    values,
    read_keys,
    log_decay,
    entering,
    carried,
    within,
    gate_rows,
    skip_gain,
    norm_gain,
):
    tokens, heads, head = values.shape
    count = tokens // BLOCK
    cum = jnp.cumsum(log_decay.reshape(count, BLOCK, heads), axis=1)
    block_total = cum[:, -1, :]
    before = jnp.cumsum(block_total, axis=0) - block_total
    states = entering + jnp.exp(before)[:, :, None, None] * carried[None]
    reads = read_keys.reshape(count, BLOCK, -1)
    blocked = values.reshape(count, BLOCK, heads, head)
    across = jnp.exp(cum)[..., None] * jnp.einsum(
        "ctn,chpn->cthp", reads, states.astype(jnp.bfloat16), preferred_element_type=jnp.float32
    )
    mixed = within + across + skip_gain[None, None, :, None] * blocked
    gated = mixed * jax.nn.silu(gate_rows)
    scale = lax.rsqrt(jnp.mean(gated * gated, axis=(2, 3), keepdims=True) + EPS)
    return (gated * scale * norm_gain.reshape(heads, head)[None, None]).astype(jnp.bfloat16)


def carry_weights(logs, backward):
    parts = logs.shape[1]
    inclusive = jnp.cumsum(logs, axis=1)
    exclusive = inclusive - logs
    rows = lax.broadcasted_iota(jnp.int32, (parts, parts), 0)
    cols = lax.broadcasted_iota(jnp.int32, (parts, parts), 1)
    if backward:
        keep = (cols > rows)[None]
        power = exclusive[:, None, :] - inclusive[:, :, None]
    else:
        keep = (cols < rows)[None]
        power = exclusive[:, :, None] - inclusive[:, None, :]
    return jnp.where(keep, jnp.exp(jnp.where(keep, power, 0.0)), 0.0)


def settle_forward(pieces):
    states_in, totals_in = pieces
    weights = carry_weights(totals_in[:, :, 0], False)
    settled = jnp.einsum("hij,hjw->hiw", weights, states_in, precision=HIGH)
    return lax.all_to_all(settled, "seq", split_axis=1, concat_axis=1, tiled=True)


def settle_backward(pieces):
    states_in, totals_in = pieces
    weights = carry_weights(totals_in[:, :, 0], True)
    settled = jnp.einsum("hij,hjw->hiw", weights, states_in, precision=HIGH)
    return lax.all_to_all(settled, "seq", split_axis=1, concat_axis=1, tiled=True)


def spread_sum(flat, axes):
    count = 1
    for axis in axes:
        count *= lax.axis_size(axis)
    size = flat.shape[0]
    chunk = -(-size // count)
    padded = jnp.pad(flat, (0, chunk * count - size)).reshape(count, chunk)
    gathered = lax.all_to_all(padded, axes, split_axis=0, concat_axis=0, tiled=True)
    reduced = jnp.sum(gathered, axis=0, keepdims=True)
    spread = jnp.broadcast_to(reduced, (count, chunk))
    whole = lax.all_to_all(spread, axes, split_axis=0, concat_axis=0, tiled=True)
    return whole.reshape(-1)[:size]


def local(
    token_ids,
    input_table,
    gate_table,
    step_table,
    decay_log,
    conv_weight,
    conv_bias,
    skip_gain,
    norm_gain,
    cotangent,
):
    labels = token_ids[0]
    tokens = labels.shape[0]
    width = conv_weight.shape[0]
    vocab = input_table.shape[0]
    inner = gate_table.shape[1]
    heads = step_table.shape[1]
    rim = shifted(labels[tokens - width + 1 :] + 1, "seq", 1) - 1
    extended = jnp.concatenate([rim, labels])
    wide_hot = indicator(extended, vocab, jnp.bfloat16)
    own_hot = wide_hot[width - 1 :]
    raw_rows = jnp.dot(wide_hot, input_table, preferred_element_type=jnp.float32)
    gate_rows = jnp.dot(own_hot, gate_table, preferred_element_type=jnp.float32)
    step_rows = jnp.dot(own_hot.astype(jnp.float32), step_table, precision=HIGH)
    features, pull_prepare = jax.vjp(
        partial(prepare, inner=inner, heads=heads),
        raw_rows,
        step_rows,
        decay_log,
        conv_weight,
        conv_bias,
    )
    values, write_keys, read_keys, steps, log_decay = features
    pieces, pull_groups = jax.vjp(group_states, values, write_keys, steps, log_decay)
    (entering, final, total), pull_local = jax.vjp(local_states, pieces, log_decay)
    flat = final.reshape(heads, -1)
    parts = lax.axis_size("seq")
    span = flat.shape[1] // parts
    total_row = jnp.zeros((1, parts, span), jnp.float32).at[0, :, :heads].set(
        jnp.broadcast_to(total[None, :], (parts, heads))
    )
    outgoing = jnp.concatenate([flat.reshape(heads, parts, span), total_row], axis=0)
    within, pull_intra = jax.vjp(intra, values, write_keys, read_keys, steps, log_decay)
    incoming = lax.all_to_all(outgoing, "seq", split_axis=1, concat_axis=1, tiled=True)
    count = tokens // BLOCK
    head = inner // heads
    gate_view = gate_rows.reshape(count, BLOCK, heads, head)
    cot_view = cotangent[0].reshape(count, BLOCK, heads, head)
    incoming, within, gate_view, cot_view = lax.optimization_barrier(
        (incoming, within, gate_view, cot_view)
    )
    totals = jnp.transpose(incoming[heads, :, :heads])[:, :, None]
    carried = settle_forward((incoming[:heads], totals))
    layer_out, pull_out = jax.vjp(
        mixer_output,
        values,
        read_keys,
        log_decay,
        entering,
        carried,
        within,
        gate_view,
        skip_gain,
        norm_gain,
    )
    d_values, d_read, d_log, d_entering, d_carried, d_within, d_gate, d_skip, d_norm = pull_out(
        cot_view
    )
    d_gate = d_gate.reshape(tokens, inner)
    back_flat = d_carried.reshape(heads, -1)
    back_incoming = lax.all_to_all(
        back_flat.reshape(heads, parts, span), "seq", split_axis=1, concat_axis=1, tiled=True
    )
    d_intra = pull_intra(d_within)
    back_incoming, d_intra = lax.optimization_barrier((back_incoming, d_intra))
    later = settle_backward((back_incoming, totals))
    d_total = jnp.exp(total) * jnp.sum(later * carried, axis=(1, 2))
    d_pieces, d_log_local = pull_local((d_entering, later, d_total))
    d_values_state, d_write_state, d_steps_state, d_log_state = pull_groups(d_pieces)
    d_raw, d_step_rows, d_decay, d_taps, d_shift = pull_prepare(
        (
            d_values + d_intra[0] + d_values_state,
            d_intra[1] + d_write_state,
            d_read + d_intra[2],
            d_intra[3] + d_steps_state,
            d_log + d_intra[4] + d_log_state + d_log_local,
        )
    )
    wide_float = wide_hot.astype(jnp.float32)
    own_float = wide_float[width - 1 :]
    parts_list = (
        jnp.dot(wide_float.T, d_raw, precision=HIGH),
        jnp.dot(own_float.T, d_gate, precision=HIGH),
        jnp.dot(own_float.T, d_step_rows, precision=HIGH),
        d_decay,
        d_taps,
        d_shift,
        d_skip,
        d_norm,
    )
    packed = jnp.concatenate([part.reshape(-1) for part in parts_list])
    packed = spread_sum(packed, ("seq", "batch"))
    sums = []
    offset = 0
    for part in parts_list:
        sums.append(packed[offset : offset + part.size].reshape(part.shape))
        offset += part.size
    return (layer_out.reshape(1, tokens, inner), sums[0], sums[1], sums[2], sums[3], sums[4], sums[5], sums[6], sums[7])


def solution(mesh):
    return jax.shard_map(
        local,
        mesh=mesh,
        in_specs=(
            P("batch", "seq"),
            P(),
            P(),
            P(),
            P(),
            P(),
            P(),
            P(),
            P(),
            P("batch", "seq", None),
        ),
        out_specs=(P("batch", "seq", None), P(), P(), P(), P(), P(), P(), P(), P()),
        check_vma=False,
    )
```

```python
from functools import partial

import jax
import jax.numpy as jnp
from jax import lax
from jax.sharding import PartitionSpec as P

BLOCK = 128


EPS = 1e-05
HIGH = lax.Precision.HIGHEST


def shifted(value, axis, steps):
    count = lax.axis_size(axis)
    leading, last = (max(0, -steps), min(count, count - steps))
    return lax.ppermute(value, axis, [(source, source + steps) for source in range(leading, last)])


def indicator(labels, vocab, kind):
    return (labels[:, None] == jnp.arange(vocab, dtype=jnp.int32)[None, :]).astype(kind)


def convolve(raw_rows, conv_weight, conv_bias):
    width = conv_weight.shape[0]
    tokens = raw_rows.shape[0] - width + 1
    convolved = conv_bias[None, :] + conv_weight[0][None, :] * raw_rows[0:tokens]
    for offset in range(1, width):
        convolved = convolved + conv_weight[offset][None, :] * raw_rows[offset : offset + tokens]
    return convolved


def prepare(convolved, step_rows, decay_log, inner, heads):
    tokens = convolved.shape[0]
    state = (convolved.shape[1] - inner) // 2
    active = jax.nn.silu(convolved)
    values = active[:, :inner].astype(jnp.bfloat16).reshape(tokens, heads, inner // heads)
    write_keys = active[:, inner : inner + state].astype(jnp.bfloat16)
    read_keys = active[:, inner + state :].astype(jnp.bfloat16)
    steps = jax.nn.softplus(step_rows)
    log_decay = -jnp.exp(decay_log)[None, :] * steps
    return (values, write_keys, read_keys, steps, log_decay)


def group_states(values, write_keys, steps, log_decay):
    tokens, heads, head = values.shape
    count = tokens // BLOCK
    cum = jnp.cumsum(log_decay.reshape(count, BLOCK, heads), axis=1)
    factor = jnp.exp(cum[:, -1:, :] - cum) * steps.reshape(count, BLOCK, heads)
    weighted = (values.reshape(count, BLOCK, heads, head) * factor[..., None]).astype(jnp.bfloat16)
    return jnp.einsum(
        "cshp,csn->chpn",
        weighted,
        write_keys.reshape(count, BLOCK, -1),
        preferred_element_type=jnp.float32,
    )


def local_states(pieces, log_decay):
    count = pieces.shape[0]
    block_total = jnp.sum(log_decay.reshape(count, BLOCK, -1), axis=1)

    def advance(carried, item):
        piece, total = item
        return (jnp.exp(total)[:, None, None] * carried + piece, carried)

    final, entering = lax.scan(
        advance, jnp.zeros_like(pieces[0]), (pieces, block_total), unroll=True
    )
    return (entering, final, jnp.sum(block_total, axis=0))


def intra(values, write_keys, read_keys, steps, log_decay):
    tokens, heads, head = values.shape
    count = tokens // BLOCK
    cum = jnp.cumsum(log_decay.reshape(count, BLOCK, heads), axis=1)
    writes = write_keys.reshape(count, BLOCK, -1)
    reads = read_keys.reshape(count, BLOCK, -1)
    scores = jnp.einsum("ctn,csn->cts", reads, writes, preferred_element_type=jnp.float32)
    lower = (
        lax.broadcasted_iota(jnp.int32, (BLOCK, BLOCK), 0)
        >= lax.broadcasted_iota(jnp.int32, (BLOCK, BLOCK), 1)
    )[None, None]
    track = jnp.transpose(cum, (0, 2, 1))
    power = track[:, :, :, None] - track[:, :, None, :]
    fade = jnp.where(lower, jnp.exp(jnp.where(lower, power, 0.0)), 0.0)
    widths = jnp.transpose(steps.reshape(count, BLOCK, heads), (0, 2, 1))
    mixing = (scores[:, None] * fade * widths[:, :, None, :]).astype(jnp.bfloat16)
    blocked = values.reshape(count, BLOCK, heads, head)
    return jnp.einsum("chts,cshp->cthp", mixing, blocked, preferred_element_type=jnp.float32)


def mixer_output(
    values,
    read_keys,
    log_decay,
    entering,
    carried,
    within,
    gate_rows,
    skip_gain,
    norm_gain,
):
    tokens, heads, head = values.shape
    count = tokens // BLOCK
    cum = jnp.cumsum(log_decay.reshape(count, BLOCK, heads), axis=1)
    block_total = cum[:, -1, :]
    before = jnp.cumsum(block_total, axis=0) - block_total
    states = entering + jnp.exp(before)[:, :, None, None] * carried[None]
    reads = read_keys.reshape(count, BLOCK, -1)
    blocked = values.reshape(count, BLOCK, heads, head)
    across = jnp.exp(cum)[..., None] * jnp.einsum(
        "ctn,chpn->cthp", reads, states.astype(jnp.bfloat16), preferred_element_type=jnp.float32
    )
    mixed = within + across + skip_gain[None, None, :, None] * blocked
    gated = mixed * jax.nn.silu(gate_rows)
    scale = lax.rsqrt(jnp.mean(gated * gated, axis=(2, 3), keepdims=True) + EPS)
    return (gated * scale * norm_gain.reshape(heads, head)[None, None]).astype(jnp.bfloat16)


def carry_weights(logs, backward):
    parts = logs.shape[1]
    inclusive = jnp.cumsum(logs, axis=1)
    exclusive = inclusive - logs
    rows = lax.broadcasted_iota(jnp.int32, (parts, parts), 0)
    cols = lax.broadcasted_iota(jnp.int32, (parts, parts), 1)
    if backward:
        keep = (cols > rows)[None]
        power = exclusive[:, None, :] - inclusive[:, :, None]
    else:
        keep = (cols < rows)[None]
        power = exclusive[:, :, None] - inclusive[:, None, :]
    return jnp.where(keep, jnp.exp(jnp.where(keep, power, 0.0)), 0.0)


def settle_forward(pieces):
    states_in, totals_in = pieces
    weights = carry_weights(totals_in[:, :, 0], False)
    settled = jnp.einsum("hij,hjw->hiw", weights, states_in, precision=HIGH)
    return lax.all_to_all(settled, "seq", split_axis=1, concat_axis=1, tiled=True)


def settle_backward(pieces):
    states_in, totals_in = pieces
    weights = carry_weights(totals_in[:, :, 0], True)
    settled = jnp.einsum("hij,hjw->hiw", weights, states_in, precision=HIGH)
    return lax.all_to_all(settled, "seq", split_axis=1, concat_axis=1, tiled=True)


def spread_sum(flat, axes):
    count = 1
    for axis in axes:
        count *= lax.axis_size(axis)
    size = flat.shape[0]
    chunk = -(-size // count)
    padded = jnp.pad(flat, (0, chunk * count - size)).reshape(count, chunk)
    gathered = lax.all_to_all(padded, axes, split_axis=0, concat_axis=0, tiled=True)
    reduced = jnp.sum(gathered, axis=0, keepdims=True)
    spread = jnp.broadcast_to(reduced, (count, chunk))
    whole = lax.all_to_all(spread, axes, split_axis=0, concat_axis=0, tiled=True)
    return whole.reshape(-1)[:size]


def local(
    token_ids,
    input_table,
    gate_table,
    step_table,
    decay_log,
    conv_weight,
    conv_bias,
    skip_gain,
    norm_gain,
    cotangent,
):
    labels = token_ids[0]
    tokens = labels.shape[0]
    width = conv_weight.shape[0]
    vocab = input_table.shape[0]
    inner = gate_table.shape[1]
    heads = step_table.shape[1]
    rim = shifted(labels[tokens - width + 1 :] + 1, "seq", 1) - 1
    extended = jnp.concatenate([rim, labels])
    wide_hot = indicator(extended, vocab, jnp.bfloat16)
    own_hot = wide_hot[width - 1 :]
    raw_rows = jnp.dot(wide_hot, input_table, preferred_element_type=jnp.float32)
    gate_rows = jnp.dot(own_hot, gate_table, preferred_element_type=jnp.float32)
    step_rows = jnp.dot(own_hot.astype(jnp.float32), step_table, precision=HIGH)
    convolved = convolve(raw_rows, conv_weight, conv_bias)
    features, pull_prepare = jax.vjp(
        partial(prepare, inner=inner, heads=heads),
        convolved,
        step_rows,
        decay_log,
    )
    values, write_keys, read_keys, steps, log_decay = features
    pieces, pull_groups = jax.vjp(group_states, values, write_keys, steps, log_decay)
    (entering, final, total), pull_local = jax.vjp(local_states, pieces, log_decay)
    flat = final.reshape(heads, -1)
    parts = lax.axis_size("seq")
    span = flat.shape[1] // parts
    total_row = jnp.zeros((1, parts, span), jnp.float32).at[0, :, :heads].set(
        jnp.broadcast_to(total[None, :], (parts, heads))
    )
    outgoing = jnp.concatenate([flat.reshape(heads, parts, span), total_row], axis=0)
    within, pull_intra = jax.vjp(intra, values, write_keys, read_keys, steps, log_decay)
    incoming = lax.all_to_all(outgoing, "seq", split_axis=1, concat_axis=1, tiled=True)
    count = tokens // BLOCK
    head = inner // heads
    gate_view = gate_rows.reshape(count, BLOCK, heads, head)
    cot_view = cotangent[0].reshape(count, BLOCK, heads, head)
    incoming, within, gate_view, cot_view = lax.optimization_barrier(
        (incoming, within, gate_view, cot_view)
    )
    totals = jnp.transpose(incoming[heads, :, :heads])[:, :, None]
    carried = settle_forward((incoming[:heads], totals))
    layer_out, pull_out = jax.vjp(
        mixer_output,
        values,
        read_keys,
        log_decay,
        entering,
        carried,
        within,
        gate_view,
        skip_gain,
        norm_gain,
    )
    d_values, d_read, d_log, d_entering, d_carried, d_within, d_gate, d_skip, d_norm = pull_out(
        cot_view
    )
    d_gate = d_gate.reshape(tokens, inner)
    back_flat = d_carried.reshape(heads, -1)
    back_incoming = lax.all_to_all(
        back_flat.reshape(heads, parts, span), "seq", split_axis=1, concat_axis=1, tiled=True
    )
    d_intra = pull_intra(d_within)
    back_incoming, d_intra = lax.optimization_barrier((back_incoming, d_intra))
    later = settle_backward((back_incoming, totals))
    d_total = jnp.exp(total) * jnp.sum(later * carried, axis=(1, 2))
    d_pieces, d_log_local = pull_local((d_entering, later, d_total))
    d_values_state, d_write_state, d_steps_state, d_log_state = pull_groups(d_pieces)
    d_conv, d_step_rows, d_decay = pull_prepare(
        (
            d_values + d_intra[0] + d_values_state,
            d_intra[1] + d_write_state,
            d_read + d_intra[2],
            d_intra[3] + d_steps_state,
            d_log + d_intra[4] + d_log_state + d_log_local,
        )
    )
    wide_float = wide_hot.astype(jnp.float32)
    own_float = wide_float[width - 1 :]
    shifted_hot = jnp.concatenate(
        [wide_float[offset : offset + tokens].T for offset in range(width)], axis=0
    )
    per_tap = jnp.dot(shifted_hot, d_conv, precision=HIGH).reshape(width, vocab, -1)
    table_grad = jnp.sum(conv_weight[:, None, :] * per_tap, axis=0)
    d_taps = jnp.sum(input_table.astype(jnp.float32)[None] * per_tap, axis=1)
    d_shift = jnp.sum(d_conv, axis=0)
    parts_list = (
        table_grad,
        jnp.dot(own_float.T, d_gate, precision=HIGH),
        jnp.dot(own_float.T, d_step_rows, precision=HIGH),
        d_decay,
        d_taps,
        d_shift,
        d_skip,
        d_norm,
    )
    packed = jnp.concatenate([part.reshape(-1) for part in parts_list])
    packed = spread_sum(packed, ("seq", "batch"))
    sums = []
    offset = 0
    for part in parts_list:
        sums.append(packed[offset : offset + part.size].reshape(part.shape))
        offset += part.size
    return (layer_out.reshape(1, tokens, inner), sums[0], sums[1], sums[2], sums[3], sums[4], sums[5], sums[6], sums[7])


def solution(mesh):
    return jax.shard_map(
        local,
        mesh=mesh,
        in_specs=(
            P("batch", "seq"),
            P(),
            P(),
            P(),
            P(),
            P(),
            P(),
            P(),
            P(),
            P("batch", "seq", None),
        ),
        out_specs=(P("batch", "seq", None), P(), P(), P(), P(), P(), P(), P(), P()),
        check_vma=False,
    )
```

```python
from functools import partial

import jax
import jax.numpy as jnp
from jax import lax
from jax.sharding import PartitionSpec as P

BLOCK = 128


EPS = 1e-05
HIGH = lax.Precision.HIGH


def shifted(value, axis, steps):
    count = lax.axis_size(axis)
    leading, last = (max(0, -steps), min(count, count - steps))
    return lax.ppermute(value, axis, [(source, source + steps) for source in range(leading, last)])


def indicator(labels, vocab, kind):
    return (labels[:, None] == jnp.arange(vocab, dtype=jnp.int32)[None, :]).astype(kind)


def convolve(raw_rows, conv_weight, conv_bias):
    width = conv_weight.shape[0]
    tokens = raw_rows.shape[0] - width + 1
    convolved = conv_bias[None, :] + conv_weight[0][None, :] * raw_rows[0:tokens]
    for offset in range(1, width):
        convolved = convolved + conv_weight[offset][None, :] * raw_rows[offset : offset + tokens]
    return convolved


def prepare(convolved, step_rows, decay_log, inner, heads):
    tokens = convolved.shape[0]
    state = (convolved.shape[1] - inner) // 2
    active = jax.nn.silu(convolved)
    values = active[:, :inner].astype(jnp.bfloat16).reshape(tokens, heads, inner // heads)
    write_keys = active[:, inner : inner + state].astype(jnp.bfloat16)
    read_keys = active[:, inner + state :].astype(jnp.bfloat16)
    steps = jax.nn.softplus(step_rows)
    log_decay = -jnp.exp(decay_log)[None, :] * steps
    return (values, write_keys, read_keys, steps, log_decay)


def group_states(values, write_keys, steps, log_decay):
    tokens, heads, head = values.shape
    count = tokens // BLOCK
    cum = jnp.cumsum(log_decay.reshape(count, BLOCK, heads), axis=1)
    factor = jnp.exp(cum[:, -1:, :] - cum) * steps.reshape(count, BLOCK, heads)
    weighted = (values.reshape(count, BLOCK, heads, head) * factor[..., None]).astype(jnp.bfloat16)
    return jnp.einsum(
        "cshp,csn->chpn",
        weighted,
        write_keys.reshape(count, BLOCK, -1),
        preferred_element_type=jnp.float32,
    )


def local_states(pieces, log_decay):
    count = pieces.shape[0]
    block_total = jnp.sum(log_decay.reshape(count, BLOCK, -1), axis=1)

    def advance(carried, item):
        piece, total = item
        return (jnp.exp(total)[:, None, None] * carried + piece, carried)

    final, entering = lax.scan(
        advance, jnp.zeros_like(pieces[0]), (pieces, block_total), unroll=True
    )
    return (entering, final, jnp.sum(block_total, axis=0))


def intra(values, write_keys, read_keys, steps, log_decay):
    tokens, heads, head = values.shape
    count = tokens // BLOCK
    cum = jnp.cumsum(log_decay.reshape(count, BLOCK, heads), axis=1)
    writes = write_keys.reshape(count, BLOCK, -1)
    reads = read_keys.reshape(count, BLOCK, -1)
    scores = jnp.einsum("ctn,csn->cts", reads, writes, preferred_element_type=jnp.float32)
    lower = (
        lax.broadcasted_iota(jnp.int32, (BLOCK, BLOCK), 0)
        >= lax.broadcasted_iota(jnp.int32, (BLOCK, BLOCK), 1)
    )[None, None]
    track = jnp.transpose(cum, (0, 2, 1))
    power = track[:, :, :, None] - track[:, :, None, :]
    fade = jnp.where(lower, jnp.exp(jnp.where(lower, power, 0.0)), 0.0)
    widths = jnp.transpose(steps.reshape(count, BLOCK, heads), (0, 2, 1))
    mixing = (scores[:, None] * fade * widths[:, :, None, :]).astype(jnp.bfloat16)
    blocked = values.reshape(count, BLOCK, heads, head)
    return jnp.einsum("chts,cshp->cthp", mixing, blocked, preferred_element_type=jnp.float32)


def mixer_output(
    values,
    read_keys,
    log_decay,
    entering,
    carried,
    within,
    gate_rows,
    skip_gain,
    norm_gain,
):
    tokens, heads, head = values.shape
    count = tokens // BLOCK
    cum = jnp.cumsum(log_decay.reshape(count, BLOCK, heads), axis=1)
    block_total = cum[:, -1, :]
    before = jnp.cumsum(block_total, axis=0) - block_total
    states = entering + jnp.exp(before)[:, :, None, None] * carried[None]
    reads = read_keys.reshape(count, BLOCK, -1)
    blocked = values.reshape(count, BLOCK, heads, head)
    across = jnp.exp(cum)[..., None] * jnp.einsum(
        "ctn,chpn->cthp", reads, states.astype(jnp.bfloat16), preferred_element_type=jnp.float32
    )
    mixed = within + across + skip_gain[None, None, :, None] * blocked
    gated = mixed * jax.nn.silu(gate_rows)
    scale = lax.rsqrt(jnp.mean(gated * gated, axis=(2, 3), keepdims=True) + EPS)
    return (gated * scale * norm_gain.reshape(heads, head)[None, None]).astype(jnp.bfloat16)


def carry_weights(logs, backward):
    parts = logs.shape[1]
    inclusive = jnp.cumsum(logs, axis=1)
    exclusive = inclusive - logs
    rows = lax.broadcasted_iota(jnp.int32, (parts, parts), 0)
    cols = lax.broadcasted_iota(jnp.int32, (parts, parts), 1)
    if backward:
        keep = (cols > rows)[None]
        power = exclusive[:, None, :] - inclusive[:, :, None]
    else:
        keep = (cols < rows)[None]
        power = exclusive[:, :, None] - inclusive[:, None, :]
    return jnp.where(keep, jnp.exp(jnp.where(keep, power, 0.0)), 0.0)


def settle_forward(pieces):
    states_in, totals_in = pieces
    weights = carry_weights(totals_in[:, :, 0], False)
    settled = jnp.einsum("hij,hjw->hiw", weights, states_in, precision=HIGH)
    return lax.all_to_all(settled, "seq", split_axis=1, concat_axis=1, tiled=True)


def settle_backward(pieces):
    states_in, totals_in = pieces
    weights = carry_weights(totals_in[:, :, 0], True)
    settled = jnp.einsum("hij,hjw->hiw", weights, states_in, precision=HIGH)
    return lax.all_to_all(settled, "seq", split_axis=1, concat_axis=1, tiled=True)


def spread_sum(flat, axes):
    count = 1
    for axis in axes:
        count *= lax.axis_size(axis)
    size = flat.shape[0]
    chunk = -(-size // count)
    padded = jnp.pad(flat, (0, chunk * count - size)).reshape(count, chunk)
    gathered = lax.all_to_all(padded, axes, split_axis=0, concat_axis=0, tiled=True)
    reduced = jnp.sum(gathered, axis=0, keepdims=True)
    spread = jnp.broadcast_to(reduced, (count, chunk))
    whole = lax.all_to_all(spread, axes, split_axis=0, concat_axis=0, tiled=True)
    return whole.reshape(-1)[:size]


def local(
    token_ids,
    input_table,
    gate_table,
    step_table,
    decay_log,
    conv_weight,
    conv_bias,
    skip_gain,
    norm_gain,
    cotangent,
):
    labels = token_ids[0]
    tokens = labels.shape[0]
    width = conv_weight.shape[0]
    vocab = input_table.shape[0]
    inner = gate_table.shape[1]
    heads = step_table.shape[1]
    rim = shifted(labels[tokens - width + 1 :] + 1, "seq", 1) - 1
    extended = jnp.concatenate([rim, labels])
    wide_hot = indicator(extended, vocab, jnp.bfloat16)
    own_hot = wide_hot[width - 1 :]
    raw_rows = jnp.dot(wide_hot, input_table, preferred_element_type=jnp.float32)
    gate_rows = jnp.dot(own_hot, gate_table, preferred_element_type=jnp.float32)
    step_rows = jnp.dot(own_hot.astype(jnp.float32), step_table, precision=HIGH)
    convolved = convolve(raw_rows, conv_weight, conv_bias)
    features, pull_prepare = jax.vjp(
        partial(prepare, inner=inner, heads=heads),
        convolved,
        step_rows,
        decay_log,
    )
    values, write_keys, read_keys, steps, log_decay = features
    pieces, pull_groups = jax.vjp(group_states, values, write_keys, steps, log_decay)
    (entering, final, total), pull_local = jax.vjp(local_states, pieces, log_decay)
    flat = final.reshape(heads, -1)
    parts = lax.axis_size("seq")
    span = flat.shape[1] // parts
    total_row = jnp.zeros((1, parts, span), jnp.float32).at[0, :, :heads].set(
        jnp.broadcast_to(total[None, :], (parts, heads))
    )
    outgoing = jnp.concatenate([flat.reshape(heads, parts, span), total_row], axis=0)
    within, pull_intra = jax.vjp(intra, values, write_keys, read_keys, steps, log_decay)
    incoming = lax.all_to_all(outgoing, "seq", split_axis=1, concat_axis=1, tiled=True)
    count = tokens // BLOCK
    head = inner // heads
    gate_view = gate_rows.reshape(count, BLOCK, heads, head)
    cot_view = cotangent[0].reshape(count, BLOCK, heads, head)
    incoming, within, gate_view, cot_view = lax.optimization_barrier(
        (incoming, within, gate_view, cot_view)
    )
    totals = jnp.transpose(incoming[heads, :, :heads])[:, :, None]
    carried = settle_forward((incoming[:heads], totals))
    layer_out, pull_out = jax.vjp(
        mixer_output,
        values,
        read_keys,
        log_decay,
        entering,
        carried,
        within,
        gate_view,
        skip_gain,
        norm_gain,
    )
    d_values, d_read, d_log, d_entering, d_carried, d_within, d_gate, d_skip, d_norm = pull_out(
        cot_view
    )
    d_gate = d_gate.reshape(tokens, inner)
    back_flat = d_carried.reshape(heads, -1)
    back_incoming = lax.all_to_all(
        back_flat.reshape(heads, parts, span), "seq", split_axis=1, concat_axis=1, tiled=True
    )
    d_intra = pull_intra(d_within)
    back_incoming, d_intra = lax.optimization_barrier((back_incoming, d_intra))
    later = settle_backward((back_incoming, totals))
    d_total = jnp.exp(total) * jnp.sum(later * carried, axis=(1, 2))
    d_pieces, d_log_local = pull_local((d_entering, later, d_total))
    d_values_state, d_write_state, d_steps_state, d_log_state = pull_groups(d_pieces)
    d_conv, d_step_rows, d_decay = pull_prepare(
        (
            d_values + d_intra[0] + d_values_state,
            d_intra[1] + d_write_state,
            d_read + d_intra[2],
            d_intra[3] + d_steps_state,
            d_log + d_intra[4] + d_log_state + d_log_local,
        )
    )
    wide_float = wide_hot.astype(jnp.float32)
    own_float = wide_float[width - 1 :]
    shifted_hot = jnp.concatenate(
        [wide_float[offset : offset + tokens].T for offset in range(width)], axis=0
    )
    per_tap = jnp.dot(shifted_hot, d_conv, precision=HIGH).reshape(width, vocab, -1)
    table_grad = jnp.sum(conv_weight[:, None, :] * per_tap, axis=0)
    d_taps = jnp.sum(input_table.astype(jnp.float32)[None] * per_tap, axis=1)
    d_shift = jnp.sum(d_conv, axis=0)
    parts_list = (
        table_grad,
        jnp.dot(own_float.T, d_gate, precision=HIGH),
        jnp.dot(own_float.T, d_step_rows, precision=HIGH),
        d_decay,
        d_taps,
        d_shift,
        d_skip,
        d_norm,
    )
    packed = jnp.concatenate([part.reshape(-1) for part in parts_list])
    packed = spread_sum(packed, ("seq", "batch"))
    sums = []
    offset = 0
    for part in parts_list:
        sums.append(packed[offset : offset + part.size].reshape(part.shape))
        offset += part.size
    return (layer_out.reshape(1, tokens, inner), sums[0], sums[1], sums[2], sums[3], sums[4], sums[5], sums[6], sums[7])


def solution(mesh):
    return jax.shard_map(
        local,
        mesh=mesh,
        in_specs=(
            P("batch", "seq"),
            P(),
            P(),
            P(),
            P(),
            P(),
            P(),
            P(),
            P(),
            P("batch", "seq", None),
        ),
        out_specs=(P("batch", "seq", None), P(), P(), P(), P(), P(), P(), P(), P()),
        check_vma=False,
    )
```

```python
from functools import partial

import jax
import jax.numpy as jnp
from jax import lax
from jax.sharding import PartitionSpec as P

BLOCK = 128


EPS = 1e-05
HIGH = lax.Precision.HIGH


def shifted(value, axis, steps):
    count = lax.axis_size(axis)
    leading, last = (max(0, -steps), min(count, count - steps))
    return lax.ppermute(value, axis, [(source, source + steps) for source in range(leading, last)])


def indicator(labels, vocab, kind):
    return (labels[:, None] == jnp.arange(vocab, dtype=jnp.int32)[None, :]).astype(kind)


def convolve(raw_rows, conv_weight, conv_bias):
    width = conv_weight.shape[0]
    tokens = raw_rows.shape[0] - width + 1
    convolved = conv_bias[None, :] + conv_weight[0][None, :] * raw_rows[0:tokens]
    for offset in range(1, width):
        convolved = convolved + conv_weight[offset][None, :] * raw_rows[offset : offset + tokens]
    return convolved


def prepare(convolved, step_rows, decay_log, inner, heads):
    tokens = convolved.shape[0]
    state = (convolved.shape[1] - inner) // 2
    active = jax.nn.silu(convolved)
    values = active[:, :inner].astype(jnp.bfloat16).reshape(tokens, heads, inner // heads)
    write_keys = active[:, inner : inner + state].astype(jnp.bfloat16)
    read_keys = active[:, inner + state :].astype(jnp.bfloat16)
    steps = jax.nn.softplus(step_rows)
    log_decay = -jnp.exp(decay_log)[None, :] * steps
    return (values, write_keys, read_keys, steps, log_decay)


def group_states(values, write_keys, steps, log_decay):
    tokens, heads, head = values.shape
    count = tokens // BLOCK
    cum = jnp.cumsum(log_decay.reshape(count, BLOCK, heads), axis=1)
    factor = jnp.exp(cum[:, -1:, :] - cum) * steps.reshape(count, BLOCK, heads)
    weighted = (values.reshape(count, BLOCK, heads, head) * factor[..., None]).astype(jnp.bfloat16)
    return jnp.einsum(
        "cshp,csn->chpn",
        weighted,
        write_keys.reshape(count, BLOCK, -1),
        preferred_element_type=jnp.float32,
    )


def local_states(pieces, log_decay):
    count = pieces.shape[0]
    block_total = jnp.sum(log_decay.reshape(count, BLOCK, -1), axis=1)

    def advance(carried, item):
        piece, total = item
        return (jnp.exp(total)[:, None, None] * carried + piece, carried)

    final, entering = lax.scan(
        advance, jnp.zeros_like(pieces[0]), (pieces, block_total), unroll=True
    )
    return (entering, final, jnp.sum(block_total, axis=0))


def intra(values, write_keys, read_keys, steps, log_decay):
    tokens, heads, head = values.shape
    count = tokens // BLOCK
    cum = jnp.cumsum(log_decay.reshape(count, BLOCK, heads), axis=1)
    writes = write_keys.reshape(count, BLOCK, -1)
    reads = read_keys.reshape(count, BLOCK, -1)
    scores = jnp.einsum("ctn,csn->cts", reads, writes, preferred_element_type=jnp.float32)
    lower = (
        lax.broadcasted_iota(jnp.int32, (BLOCK, BLOCK), 0)
        >= lax.broadcasted_iota(jnp.int32, (BLOCK, BLOCK), 1)
    )[None, None]
    track = jnp.transpose(cum, (0, 2, 1))
    power = track[:, :, :, None] - track[:, :, None, :]
    fade = jnp.where(lower, jnp.exp(jnp.where(lower, power, 0.0)), 0.0)
    widths = jnp.transpose(steps.reshape(count, BLOCK, heads), (0, 2, 1))
    mixing = (scores[:, None] * fade * widths[:, :, None, :]).astype(jnp.bfloat16)
    blocked = values.reshape(count, BLOCK, heads, head)
    return jnp.einsum("chts,cshp->cthp", mixing, blocked, preferred_element_type=jnp.float32)


def mixer_output(
    values,
    read_keys,
    log_decay,
    entering,
    carried,
    within,
    gate_rows,
    skip_gain,
    norm_gain,
):
    tokens, heads, head = values.shape
    count = tokens // BLOCK
    cum = jnp.cumsum(log_decay.reshape(count, BLOCK, heads), axis=1)
    block_total = cum[:, -1, :]
    before = jnp.cumsum(block_total, axis=0) - block_total
    states = entering + jnp.exp(before)[:, :, None, None] * carried[None]
    reads = read_keys.reshape(count, BLOCK, -1)
    blocked = values.reshape(count, BLOCK, heads, head)
    across = jnp.exp(cum)[..., None] * jnp.einsum(
        "ctn,chpn->cthp", reads, states.astype(jnp.bfloat16), preferred_element_type=jnp.float32
    )
    mixed = within + across + skip_gain[None, None, :, None] * blocked
    gated = mixed * jax.nn.silu(gate_rows)
    scale = lax.rsqrt(jnp.mean(gated * gated, axis=(2, 3), keepdims=True) + EPS)
    return (gated * scale * norm_gain.reshape(heads, head)[None, None]).astype(jnp.bfloat16)


def carry_weights(logs, backward):
    parts = logs.shape[1]
    inclusive = jnp.cumsum(logs, axis=1)
    exclusive = inclusive - logs
    rows = lax.broadcasted_iota(jnp.int32, (parts, parts), 0)
    cols = lax.broadcasted_iota(jnp.int32, (parts, parts), 1)
    if backward:
        keep = (cols > rows)[None]
        power = exclusive[:, None, :] - inclusive[:, :, None]
    else:
        keep = (cols < rows)[None]
        power = exclusive[:, :, None] - inclusive[:, None, :]
    return jnp.where(keep, jnp.exp(jnp.where(keep, power, 0.0)), 0.0)


def settle_forward(pieces):
    states_in, totals_in = pieces
    weights = carry_weights(totals_in[:, :, 0], False)
    settled = jnp.einsum("hij,hjw->hiw", weights, states_in, precision=HIGH)
    return lax.all_to_all(settled, "seq", split_axis=1, concat_axis=1, tiled=True)


def settle_backward(pieces):
    states_in, totals_in = pieces
    weights = carry_weights(totals_in[:, :, 0], True)
    settled = jnp.einsum("hij,hjw->hiw", weights, states_in, precision=HIGH)
    return lax.all_to_all(settled, "seq", split_axis=1, concat_axis=1, tiled=True)


def spread_sum(flat, axes):
    sizes = [lax.axis_size(axis) for axis in axes]
    count = 1
    for size_of in sizes:
        count *= size_of
    size = flat.shape[0]
    chunk = -(-size // count)
    piece = jnp.pad(flat, (0, chunk * count - size))
    for axis, parts in zip(axes, sizes):
        rows = piece.reshape(parts, -1)
        gathered = lax.all_to_all(rows, axis, split_axis=0, concat_axis=0, tiled=True)
        piece = jnp.sum(gathered, axis=0)
    for axis, parts in reversed(list(zip(axes, sizes))):
        spread = jnp.broadcast_to(piece[None], (parts, piece.shape[0]))
        piece = lax.all_to_all(spread, axis, split_axis=0, concat_axis=0, tiled=True).reshape(-1)
    return piece[:size]


def local(
    token_ids,
    input_table,
    gate_table,
    step_table,
    decay_log,
    conv_weight,
    conv_bias,
    skip_gain,
    norm_gain,
    cotangent,
):
    labels = token_ids[0]
    tokens = labels.shape[0]
    width = conv_weight.shape[0]
    vocab = input_table.shape[0]
    inner = gate_table.shape[1]
    heads = step_table.shape[1]
    rim = shifted(labels[tokens - width + 1 :] + 1, "seq", 1) - 1
    extended = jnp.concatenate([rim, labels])
    wide_hot = indicator(extended, vocab, jnp.bfloat16)
    own_hot = wide_hot[width - 1 :]
    raw_rows = jnp.dot(wide_hot, input_table, preferred_element_type=jnp.float32)
    gate_rows = jnp.dot(own_hot, gate_table, preferred_element_type=jnp.float32)
    step_rows = jnp.dot(own_hot.astype(jnp.float32), step_table, precision=HIGH)
    convolved = convolve(raw_rows, conv_weight, conv_bias)
    features, pull_prepare = jax.vjp(
        partial(prepare, inner=inner, heads=heads),
        convolved,
        step_rows,
        decay_log,
    )
    values, write_keys, read_keys, steps, log_decay = features
    pieces, pull_groups = jax.vjp(group_states, values, write_keys, steps, log_decay)
    (entering, final, total), pull_local = jax.vjp(local_states, pieces, log_decay)
    flat = final.reshape(heads, -1)
    parts = lax.axis_size("seq")
    span = flat.shape[1] // parts
    total_row = jnp.zeros((1, parts, span), jnp.float32).at[0, :, :heads].set(
        jnp.broadcast_to(total[None, :], (parts, heads))
    )
    outgoing = jnp.concatenate([flat.reshape(heads, parts, span), total_row], axis=0)
    within, pull_intra = jax.vjp(intra, values, write_keys, read_keys, steps, log_decay)
    incoming = lax.all_to_all(outgoing, "seq", split_axis=1, concat_axis=1, tiled=True)
    count = tokens // BLOCK
    head = inner // heads
    gate_view = gate_rows.reshape(count, BLOCK, heads, head)
    cot_view = cotangent[0].reshape(count, BLOCK, heads, head)
    incoming, within, gate_view, cot_view = lax.optimization_barrier(
        (incoming, within, gate_view, cot_view)
    )
    totals = jnp.transpose(incoming[heads, :, :heads])[:, :, None]
    carried = settle_forward((incoming[:heads], totals))
    layer_out, pull_out = jax.vjp(
        mixer_output,
        values,
        read_keys,
        log_decay,
        entering,
        carried,
        within,
        gate_view,
        skip_gain,
        norm_gain,
    )
    d_values, d_read, d_log, d_entering, d_carried, d_within, d_gate, d_skip, d_norm = pull_out(
        cot_view
    )
    d_gate = d_gate.reshape(tokens, inner)
    back_flat = d_carried.reshape(heads, -1)
    back_incoming = lax.all_to_all(
        back_flat.reshape(heads, parts, span), "seq", split_axis=1, concat_axis=1, tiled=True
    )
    d_intra = pull_intra(d_within)
    back_incoming, d_intra = lax.optimization_barrier((back_incoming, d_intra))
    later = settle_backward((back_incoming, totals))
    d_total = jnp.exp(total) * jnp.sum(later * carried, axis=(1, 2))
    d_pieces, d_log_local = pull_local((d_entering, later, d_total))
    d_values_state, d_write_state, d_steps_state, d_log_state = pull_groups(d_pieces)
    d_conv, d_step_rows, d_decay = pull_prepare(
        (
            d_values + d_intra[0] + d_values_state,
            d_intra[1] + d_write_state,
            d_read + d_intra[2],
            d_intra[3] + d_steps_state,
            d_log + d_intra[4] + d_log_state + d_log_local,
        )
    )
    wide_float = wide_hot.astype(jnp.float32)
    own_float = wide_float[width - 1 :]
    shifted_hot = jnp.concatenate(
        [wide_float[offset : offset + tokens].T for offset in range(width)], axis=0
    )
    per_tap = jnp.dot(shifted_hot, d_conv, precision=HIGH).reshape(width, vocab, -1)
    table_grad = jnp.sum(conv_weight[:, None, :] * per_tap, axis=0)
    d_taps = jnp.sum(input_table.astype(jnp.float32)[None] * per_tap, axis=1)
    d_shift = jnp.sum(d_conv, axis=0)
    parts_list = (
        table_grad,
        jnp.dot(own_float.T, d_gate, precision=HIGH),
        jnp.dot(own_float.T, d_step_rows, precision=HIGH),
        d_decay,
        d_taps,
        d_shift,
        d_skip,
        d_norm,
    )
    packed = jnp.concatenate([part.reshape(-1) for part in parts_list])
    packed = spread_sum(packed, ("seq", "batch"))
    sums = []
    offset = 0
    for part in parts_list:
        sums.append(packed[offset : offset + part.size].reshape(part.shape))
        offset += part.size
    return (layer_out.reshape(1, tokens, inner), sums[0], sums[1], sums[2], sums[3], sums[4], sums[5], sums[6], sums[7])


def solution(mesh):
    return jax.shard_map(
        local,
        mesh=mesh,
        in_specs=(
            P("batch", "seq"),
            P(),
            P(),
            P(),
            P(),
            P(),
            P(),
            P(),
            P(),
            P("batch", "seq", None),
        ),
        out_specs=(P("batch", "seq", None), P(), P(), P(), P(), P(), P(), P(), P()),
        check_vma=False,
    )
```

```python
from functools import partial

import jax
import jax.numpy as jnp
from jax import lax
from jax.sharding import PartitionSpec as P

BLOCK = 128


EPS = 1e-05
HIGH = lax.Precision.HIGH


def shifted(value, axis, steps):
    count = lax.axis_size(axis)
    leading, last = (max(0, -steps), min(count, count - steps))
    return lax.ppermute(value, axis, [(source, source + steps) for source in range(leading, last)])


def indicator(labels, vocab, kind):
    return (labels[:, None] == jnp.arange(vocab, dtype=jnp.int32)[None, :]).astype(kind)


def convolve(raw_rows, conv_weight, conv_bias):
    width = conv_weight.shape[0]
    tokens = raw_rows.shape[0] - width + 1
    convolved = conv_bias[None, :] + conv_weight[0][None, :] * raw_rows[0:tokens]
    for offset in range(1, width):
        convolved = convolved + conv_weight[offset][None, :] * raw_rows[offset : offset + tokens]
    return convolved


def prepare(convolved, step_rows, decay_log, inner, heads):
    tokens = convolved.shape[0]
    state = (convolved.shape[1] - inner) // 2
    active = jax.nn.silu(convolved)
    values = active[:, :inner].astype(jnp.bfloat16).reshape(tokens, heads, inner // heads)
    write_keys = active[:, inner : inner + state].astype(jnp.bfloat16)
    read_keys = active[:, inner + state :].astype(jnp.bfloat16)
    steps = jax.nn.softplus(step_rows)
    log_decay = -jnp.exp(decay_log)[None, :] * steps
    return (values, write_keys, read_keys, steps, log_decay)


def group_states(values, write_keys, steps, log_decay):
    tokens, heads, head = values.shape
    count = tokens // BLOCK
    inner = heads * head
    cum = jnp.cumsum(log_decay.reshape(count, BLOCK, heads), axis=1)
    factor = jnp.exp(cum[:, -1:, :] - cum) * steps.reshape(count, BLOCK, heads)
    expand = (
        lax.broadcasted_iota(jnp.int32, (heads, inner), 1) // head
        == lax.broadcasted_iota(jnp.int32, (heads, inner), 0)
    ).astype(jnp.float32)
    wide = jnp.einsum("csh,hk->csk", factor, expand, precision=HIGH)
    weighted = (values.reshape(count, BLOCK, inner) * wide).astype(jnp.bfloat16)
    pieces = jnp.einsum(
        "csk,csn->ckn",
        weighted,
        write_keys.reshape(count, BLOCK, -1),
        preferred_element_type=jnp.float32,
    )
    return pieces.reshape(count, heads, head, -1)


def local_states(pieces, log_decay):
    count = pieces.shape[0]
    block_total = jnp.sum(log_decay.reshape(count, BLOCK, -1), axis=1)

    def advance(carried, item):
        piece, total = item
        return (jnp.exp(total)[:, None, None] * carried + piece, carried)

    final, entering = lax.scan(
        advance, jnp.zeros_like(pieces[0]), (pieces, block_total), unroll=True
    )
    return (entering, final, jnp.sum(block_total, axis=0))


def intra(values, write_keys, read_keys, steps, log_decay):
    tokens, heads, head = values.shape
    count = tokens // BLOCK
    cum = jnp.cumsum(log_decay.reshape(count, BLOCK, heads), axis=1)
    writes = write_keys.reshape(count, BLOCK, -1)
    reads = read_keys.reshape(count, BLOCK, -1)
    scores = jnp.einsum("ctn,csn->cts", reads, writes, preferred_element_type=jnp.float32)
    lower = (
        lax.broadcasted_iota(jnp.int32, (BLOCK, BLOCK), 0)
        >= lax.broadcasted_iota(jnp.int32, (BLOCK, BLOCK), 1)
    )[None, None]
    track = jnp.transpose(cum, (0, 2, 1))
    power = track[:, :, :, None] - track[:, :, None, :]
    fade = jnp.where(lower, jnp.exp(jnp.where(lower, power, 0.0)), 0.0)
    widths = jnp.transpose(steps.reshape(count, BLOCK, heads), (0, 2, 1))
    mixing = (scores[:, None] * fade * widths[:, :, None, :]).astype(jnp.bfloat16)
    blocked = values.reshape(count, BLOCK, heads, head)
    return jnp.einsum("chts,cshp->cthp", mixing, blocked, preferred_element_type=jnp.float32)


def mixer_output(
    values,
    read_keys,
    log_decay,
    entering,
    carried,
    within,
    gate_rows,
    skip_gain,
    norm_gain,
):
    tokens, heads, head = values.shape
    count = tokens // BLOCK
    cum = jnp.cumsum(log_decay.reshape(count, BLOCK, heads), axis=1)
    block_total = cum[:, -1, :]
    before = jnp.cumsum(block_total, axis=0) - block_total
    states = entering + jnp.exp(before)[:, :, None, None] * carried[None]
    reads = read_keys.reshape(count, BLOCK, -1)
    blocked = values.reshape(count, BLOCK, heads, head)
    across = jnp.exp(cum)[..., None] * jnp.einsum(
        "ctn,chpn->cthp", reads, states.astype(jnp.bfloat16), preferred_element_type=jnp.float32
    )
    mixed = within + across + skip_gain[None, None, :, None] * blocked
    gated = mixed * jax.nn.silu(gate_rows)
    scale = lax.rsqrt(jnp.mean(gated * gated, axis=(2, 3), keepdims=True) + EPS)
    return (gated * scale * norm_gain.reshape(heads, head)[None, None]).astype(jnp.bfloat16)


def carry_weights(logs, backward):
    parts = logs.shape[1]
    inclusive = jnp.cumsum(logs, axis=1)
    exclusive = inclusive - logs
    rows = lax.broadcasted_iota(jnp.int32, (parts, parts), 0)
    cols = lax.broadcasted_iota(jnp.int32, (parts, parts), 1)
    if backward:
        keep = (cols > rows)[None]
        power = exclusive[:, None, :] - inclusive[:, :, None]
    else:
        keep = (cols < rows)[None]
        power = exclusive[:, :, None] - inclusive[:, None, :]
    return jnp.where(keep, jnp.exp(jnp.where(keep, power, 0.0)), 0.0)


def settle_forward(pieces):
    states_in, totals_in = pieces
    weights = carry_weights(totals_in[:, :, 0], False)
    settled = jnp.einsum("hij,hjw->hiw", weights, states_in, precision=HIGH)
    return lax.all_to_all(settled, "seq", split_axis=1, concat_axis=1, tiled=True)


def settle_backward(pieces):
    states_in, totals_in = pieces
    weights = carry_weights(totals_in[:, :, 0], True)
    settled = jnp.einsum("hij,hjw->hiw", weights, states_in, precision=HIGH)
    return lax.all_to_all(settled, "seq", split_axis=1, concat_axis=1, tiled=True)


def spread_sum(flat, axes):
    count = 1
    for axis in axes:
        count *= lax.axis_size(axis)
    size = flat.shape[0]
    chunk = -(-size // count)
    padded = jnp.pad(flat, (0, chunk * count - size)).reshape(count, chunk)
    gathered = lax.all_to_all(padded, axes, split_axis=0, concat_axis=0, tiled=True)
    reduced = jnp.sum(gathered, axis=0, keepdims=True)
    spread = jnp.broadcast_to(reduced, (count, chunk))
    whole = lax.all_to_all(spread, axes, split_axis=0, concat_axis=0, tiled=True)
    return whole.reshape(-1)[:size]


def local(
    token_ids,
    input_table,
    gate_table,
    step_table,
    decay_log,
    conv_weight,
    conv_bias,
    skip_gain,
    norm_gain,
    cotangent,
):
    labels = token_ids[0]
    tokens = labels.shape[0]
    width = conv_weight.shape[0]
    vocab = input_table.shape[0]
    inner = gate_table.shape[1]
    heads = step_table.shape[1]
    rim = shifted(labels[tokens - width + 1 :] + 1, "seq", 1) - 1
    extended = jnp.concatenate([rim, labels])
    wide_hot = indicator(extended, vocab, jnp.bfloat16)
    own_hot = wide_hot[width - 1 :]
    raw_rows = jnp.dot(wide_hot, input_table, preferred_element_type=jnp.float32)
    gate_rows = jnp.dot(own_hot, gate_table, preferred_element_type=jnp.float32)
    step_rows = jnp.dot(own_hot.astype(jnp.float32), step_table, precision=HIGH)
    convolved = convolve(raw_rows, conv_weight, conv_bias)
    features, pull_prepare = jax.vjp(
        partial(prepare, inner=inner, heads=heads),
        convolved,
        step_rows,
        decay_log,
    )
    values, write_keys, read_keys, steps, log_decay = features
    pieces, pull_groups = jax.vjp(group_states, values, write_keys, steps, log_decay)
    (entering, final, total), pull_local = jax.vjp(local_states, pieces, log_decay)
    flat = final.reshape(heads, -1)
    parts = lax.axis_size("seq")
    span = flat.shape[1] // parts
    total_row = jnp.zeros((1, parts, span), jnp.float32).at[0, :, :heads].set(
        jnp.broadcast_to(total[None, :], (parts, heads))
    )
    outgoing = jnp.concatenate([flat.reshape(heads, parts, span), total_row], axis=0)
    within, pull_intra = jax.vjp(intra, values, write_keys, read_keys, steps, log_decay)
    incoming = lax.all_to_all(outgoing, "seq", split_axis=1, concat_axis=1, tiled=True)
    count = tokens // BLOCK
    head = inner // heads
    gate_view = gate_rows.reshape(count, BLOCK, heads, head)
    cot_view = cotangent[0].reshape(count, BLOCK, heads, head)
    incoming, within, gate_view, cot_view = lax.optimization_barrier(
        (incoming, within, gate_view, cot_view)
    )
    totals = jnp.transpose(incoming[heads, :, :heads])[:, :, None]
    carried = settle_forward((incoming[:heads], totals))
    layer_out, pull_out = jax.vjp(
        mixer_output,
        values,
        read_keys,
        log_decay,
        entering,
        carried,
        within,
        gate_view,
        skip_gain,
        norm_gain,
    )
    d_values, d_read, d_log, d_entering, d_carried, d_within, d_gate, d_skip, d_norm = pull_out(
        cot_view
    )
    d_gate = d_gate.reshape(tokens, inner)
    back_flat = d_carried.reshape(heads, -1)
    back_incoming = lax.all_to_all(
        back_flat.reshape(heads, parts, span), "seq", split_axis=1, concat_axis=1, tiled=True
    )
    d_intra = pull_intra(d_within)
    back_incoming, d_intra = lax.optimization_barrier((back_incoming, d_intra))
    later = settle_backward((back_incoming, totals))
    d_total = jnp.exp(total) * jnp.sum(later * carried, axis=(1, 2))
    d_pieces, d_log_local = pull_local((d_entering, later, d_total))
    d_values_state, d_write_state, d_steps_state, d_log_state = pull_groups(d_pieces)
    d_conv, d_step_rows, d_decay = pull_prepare(
        (
            d_values + d_intra[0] + d_values_state,
            d_intra[1] + d_write_state,
            d_read + d_intra[2],
            d_intra[3] + d_steps_state,
            d_log + d_intra[4] + d_log_state + d_log_local,
        )
    )
    wide_float = wide_hot.astype(jnp.float32)
    own_float = wide_float[width - 1 :]
    shifted_hot = jnp.concatenate(
        [wide_float[offset : offset + tokens].T for offset in range(width)], axis=0
    )
    per_tap = jnp.dot(shifted_hot, d_conv, precision=HIGH).reshape(width, vocab, -1)
    table_grad = jnp.sum(conv_weight[:, None, :] * per_tap, axis=0)
    d_taps = jnp.sum(input_table.astype(jnp.float32)[None] * per_tap, axis=1)
    d_shift = jnp.sum(d_conv, axis=0)
    parts_list = (
        table_grad,
        jnp.dot(own_float.T, d_gate, precision=HIGH),
        jnp.dot(own_float.T, d_step_rows, precision=HIGH),
        d_decay,
        d_taps,
        d_shift,
        d_skip,
        d_norm,
    )
    packed = jnp.concatenate([part.reshape(-1) for part in parts_list])
    packed = spread_sum(packed, ("seq", "batch"))
    sums = []
    offset = 0
    for part in parts_list:
        sums.append(packed[offset : offset + part.size].reshape(part.shape))
        offset += part.size
    return (layer_out.reshape(1, tokens, inner), sums[0], sums[1], sums[2], sums[3], sums[4], sums[5], sums[6], sums[7])


def solution(mesh):
    return jax.shard_map(
        local,
        mesh=mesh,
        in_specs=(
            P("batch", "seq"),
            P(),
            P(),
            P(),
            P(),
            P(),
            P(),
            P(),
            P(),
            P("batch", "seq", None),
        ),
        out_specs=(P("batch", "seq", None), P(), P(), P(), P(), P(), P(), P(), P()),
        check_vma=False,
    )
```

```python
from functools import partial

import jax
import jax.numpy as jnp
from jax import lax
from jax.sharding import PartitionSpec as P

BLOCK = 128


EPS = 1e-05
HIGH = lax.Precision.HIGH


def shifted(value, axis, steps):
    count = lax.axis_size(axis)
    leading, last = (max(0, -steps), min(count, count - steps))
    return lax.ppermute(value, axis, [(source, source + steps) for source in range(leading, last)])


def indicator(labels, vocab, kind):
    return (labels[:, None] == jnp.arange(vocab, dtype=jnp.int32)[None, :]).astype(kind)


def convolve(raw_rows, conv_weight, conv_bias):
    width = conv_weight.shape[0]
    tokens = raw_rows.shape[0] - width + 1
    convolved = conv_bias[None, :] + conv_weight[0][None, :] * raw_rows[0:tokens]
    for offset in range(1, width):
        convolved = convolved + conv_weight[offset][None, :] * raw_rows[offset : offset + tokens]
    return convolved


def prepare(convolved, step_rows, decay_log, inner, heads):
    tokens = convolved.shape[0]
    state = (convolved.shape[1] - inner) // 2
    active = jax.nn.silu(convolved)
    values = active[:, :inner].astype(jnp.bfloat16).reshape(tokens, heads, inner // heads)
    write_keys = active[:, inner : inner + state].astype(jnp.bfloat16)
    read_keys = active[:, inner + state :].astype(jnp.bfloat16)
    steps = jax.nn.softplus(step_rows)
    log_decay = -jnp.exp(decay_log)[None, :] * steps
    return (values, write_keys, read_keys, steps, log_decay)


def group_states(values, write_keys, steps, log_decay):
    tokens, heads, head = values.shape
    count = tokens // BLOCK
    cum = jnp.cumsum(log_decay.reshape(count, BLOCK, heads), axis=1)
    factor = jnp.exp(cum[:, -1:, :] - cum) * steps.reshape(count, BLOCK, heads)
    weighted = (values.reshape(count, BLOCK, heads, head) * factor[..., None]).astype(jnp.bfloat16)
    return jnp.einsum(
        "cshp,csn->chpn",
        weighted,
        write_keys.reshape(count, BLOCK, -1),
        preferred_element_type=jnp.float32,
    )


def local_states(pieces, log_decay):
    count = pieces.shape[0]
    block_total = jnp.sum(log_decay.reshape(count, BLOCK, -1), axis=1)

    def advance(carried, item):
        piece, total = item
        return (jnp.exp(total)[:, None, None] * carried + piece, carried)

    final, entering = lax.scan(
        advance, jnp.zeros_like(pieces[0]), (pieces, block_total), unroll=True
    )
    return (entering, final, jnp.sum(block_total, axis=0))


def intra(values, write_keys, read_keys, steps, log_decay):
    tokens, heads, head = values.shape
    count = tokens // BLOCK
    cum = jnp.cumsum(log_decay.reshape(count, BLOCK, heads), axis=1)
    writes = write_keys.reshape(count, BLOCK, -1)
    reads = read_keys.reshape(count, BLOCK, -1)
    scores = jnp.einsum("ctn,csn->cts", reads, writes, preferred_element_type=jnp.float32)
    lower = (
        lax.broadcasted_iota(jnp.int32, (BLOCK, BLOCK), 0)
        >= lax.broadcasted_iota(jnp.int32, (BLOCK, BLOCK), 1)
    )[None, None]
    track = jnp.transpose(cum, (0, 2, 1))
    power = track[:, :, :, None] - track[:, :, None, :]
    fade = jnp.where(lower, jnp.exp(jnp.where(lower, power, 0.0)), 0.0)
    widths = jnp.transpose(steps.reshape(count, BLOCK, heads), (0, 2, 1))
    mixing = (scores[:, None] * fade * widths[:, :, None, :]).astype(jnp.bfloat16)
    blocked = values.reshape(count, BLOCK, heads, head)
    return jnp.einsum("chts,cshp->cthp", mixing, blocked, preferred_element_type=jnp.float32)


def mixer_output(
    values,
    read_keys,
    log_decay,
    entering,
    carried,
    within,
    gate_rows,
    skip_gain,
    norm_gain,
):
    tokens, heads, head = values.shape
    count = tokens // BLOCK
    cum = jnp.cumsum(log_decay.reshape(count, BLOCK, heads), axis=1)
    block_total = cum[:, -1, :]
    before = jnp.cumsum(block_total, axis=0) - block_total
    states = entering + jnp.exp(before)[:, :, None, None] * carried[None]
    reads = read_keys.reshape(count, BLOCK, -1)
    blocked = values.reshape(count, BLOCK, heads, head)
    across = jnp.exp(cum)[..., None] * jnp.einsum(
        "ctn,chpn->cthp", reads, states.astype(jnp.bfloat16), preferred_element_type=jnp.float32
    )
    mixed = within + across + skip_gain[None, None, :, None] * blocked
    gated = mixed * jax.nn.silu(gate_rows)
    scale = lax.rsqrt(jnp.mean(gated * gated, axis=(2, 3), keepdims=True) + EPS)
    return (gated * scale * norm_gain.reshape(heads, head)[None, None]).astype(jnp.bfloat16)


def carry_weights(logs, backward):
    parts = logs.shape[1]
    inclusive = jnp.cumsum(logs, axis=1)
    exclusive = inclusive - logs
    rows = lax.broadcasted_iota(jnp.int32, (parts, parts), 0)
    cols = lax.broadcasted_iota(jnp.int32, (parts, parts), 1)
    if backward:
        keep = (cols > rows)[None]
        power = exclusive[:, None, :] - inclusive[:, :, None]
    else:
        keep = (cols < rows)[None]
        power = exclusive[:, :, None] - inclusive[:, None, :]
    return jnp.where(keep, jnp.exp(jnp.where(keep, power, 0.0)), 0.0)


def settle_forward(pieces):
    states_in, totals_in = pieces
    weights = carry_weights(totals_in[:, :, 0], False)
    settled = jnp.einsum("hij,hjw->hiw", weights, states_in, precision=HIGH)
    return lax.all_to_all(settled, "seq", split_axis=1, concat_axis=1, tiled=True)


def settle_backward(pieces):
    states_in, totals_in = pieces
    weights = carry_weights(totals_in[:, :, 0], True)
    settled = jnp.einsum("hij,hjw->hiw", weights, states_in, precision=HIGH)
    return lax.all_to_all(settled, "seq", split_axis=1, concat_axis=1, tiled=True)


def spread_sum(flat, axes):
    count = 1
    for axis in axes:
        count *= lax.axis_size(axis)
    size = flat.shape[0]
    chunk = -(-size // count)
    chunk = -(-chunk // 128) * 128
    padded = jnp.pad(flat, (0, chunk * count - size)).reshape(count, chunk)
    gathered = lax.all_to_all(padded, axes, split_axis=0, concat_axis=0, tiled=True)
    reduced = jnp.sum(gathered, axis=0, keepdims=True)
    spread = jnp.broadcast_to(reduced, (count, chunk))
    whole = lax.all_to_all(spread, axes, split_axis=0, concat_axis=0, tiled=True)
    return whole.reshape(-1)[:size]


def local(
    token_ids,
    input_table,
    gate_table,
    step_table,
    decay_log,
    conv_weight,
    conv_bias,
    skip_gain,
    norm_gain,
    cotangent,
):
    labels = token_ids[0]
    tokens = labels.shape[0]
    width = conv_weight.shape[0]
    vocab = input_table.shape[0]
    inner = gate_table.shape[1]
    heads = step_table.shape[1]
    rim = shifted(labels[tokens - width + 1 :] + 1, "seq", 1) - 1
    extended = jnp.concatenate([rim, labels])
    wide_hot = indicator(extended, vocab, jnp.bfloat16)
    own_hot = wide_hot[width - 1 :]
    raw_rows = jnp.dot(wide_hot, input_table, preferred_element_type=jnp.float32)
    gate_rows = jnp.dot(own_hot, gate_table, preferred_element_type=jnp.float32)
    step_rows = jnp.dot(own_hot.astype(jnp.float32), step_table, precision=HIGH)
    convolved = convolve(raw_rows, conv_weight, conv_bias)
    features, pull_prepare = jax.vjp(
        partial(prepare, inner=inner, heads=heads),
        convolved,
        step_rows,
        decay_log,
    )
    values, write_keys, read_keys, steps, log_decay = features
    pieces, pull_groups = jax.vjp(group_states, values, write_keys, steps, log_decay)
    (entering, final, total), pull_local = jax.vjp(local_states, pieces, log_decay)
    flat = final.reshape(heads, -1)
    parts = lax.axis_size("seq")
    span = flat.shape[1] // parts
    total_row = jnp.zeros((1, parts, span), jnp.float32).at[0, :, :heads].set(
        jnp.broadcast_to(total[None, :], (parts, heads))
    )
    outgoing = jnp.concatenate([flat.reshape(heads, parts, span), total_row], axis=0)
    within, pull_intra = jax.vjp(intra, values, write_keys, read_keys, steps, log_decay)
    incoming = lax.all_to_all(outgoing, "seq", split_axis=1, concat_axis=1, tiled=True)
    count = tokens // BLOCK
    head = inner // heads
    gate_view = gate_rows.reshape(count, BLOCK, heads, head)
    cot_view = cotangent[0].reshape(count, BLOCK, heads, head)
    incoming, within, gate_view, cot_view = lax.optimization_barrier(
        (incoming, within, gate_view, cot_view)
    )
    totals = jnp.transpose(incoming[heads, :, :heads])[:, :, None]
    carried = settle_forward((incoming[:heads], totals))
    layer_out, pull_out = jax.vjp(
        mixer_output,
        values,
        read_keys,
        log_decay,
        entering,
        carried,
        within,
        gate_view,
        skip_gain,
        norm_gain,
    )
    d_values, d_read, d_log, d_entering, d_carried, d_within, d_gate, d_skip, d_norm = pull_out(
        cot_view
    )
    d_gate = d_gate.reshape(tokens, inner)
    back_flat = d_carried.reshape(heads, -1)
    back_incoming = lax.all_to_all(
        back_flat.reshape(heads, parts, span), "seq", split_axis=1, concat_axis=1, tiled=True
    )
    d_intra = pull_intra(d_within)
    back_incoming, d_intra = lax.optimization_barrier((back_incoming, d_intra))
    later = settle_backward((back_incoming, totals))
    d_total = jnp.exp(total) * jnp.sum(later * carried, axis=(1, 2))
    d_pieces, d_log_local = pull_local((d_entering, later, d_total))
    d_values_state, d_write_state, d_steps_state, d_log_state = pull_groups(d_pieces)
    d_conv, d_step_rows, d_decay = pull_prepare(
        (
            d_values + d_intra[0] + d_values_state,
            d_intra[1] + d_write_state,
            d_read + d_intra[2],
            d_intra[3] + d_steps_state,
            d_log + d_intra[4] + d_log_state + d_log_local,
        )
    )
    wide_float = wide_hot.astype(jnp.float32)
    own_float = wide_float[width - 1 :]
    shifted_hot = jnp.concatenate(
        [wide_float[offset : offset + tokens].T for offset in range(width)], axis=0
    )
    per_tap = jnp.dot(shifted_hot, d_conv, precision=HIGH).reshape(width, vocab, -1)
    table_grad = jnp.sum(conv_weight[:, None, :] * per_tap, axis=0)
    d_taps = jnp.sum(input_table.astype(jnp.float32)[None] * per_tap, axis=1)
    d_shift = jnp.sum(d_conv, axis=0)
    parts_list = (
        table_grad,
        jnp.dot(own_float.T, d_gate, precision=HIGH),
        jnp.dot(own_float.T, d_step_rows, precision=HIGH),
        d_decay,
        d_taps,
        d_shift,
        d_skip,
        d_norm,
    )
    packed = jnp.concatenate([part.reshape(-1) for part in parts_list])
    packed = spread_sum(packed, ("seq", "batch"))
    sums = []
    offset = 0
    for part in parts_list:
        sums.append(packed[offset : offset + part.size].reshape(part.shape))
        offset += part.size
    return (layer_out.reshape(1, tokens, inner), sums[0], sums[1], sums[2], sums[3], sums[4], sums[5], sums[6], sums[7])


def solution(mesh):
    return jax.shard_map(
        local,
        mesh=mesh,
        in_specs=(
            P("batch", "seq"),
            P(),
            P(),
            P(),
            P(),
            P(),
            P(),
            P(),
            P(),
            P("batch", "seq", None),
        ),
        out_specs=(P("batch", "seq", None), P(), P(), P(), P(), P(), P(), P(), P()),
        check_vma=False,
    )
```
